256 devices in a mesh: dp: 64 (over x, y_hi, z), tensor: 4 (over y_lo, core).
Axes of the slice: x: 4, y: 4 (y_hi: 2, y_lo: 2; y = y_hi * 2 + y_lo), z: 8, core: 2. Of those that a mesh axis runs over, the one named last changes fastest.
Arguments:
- residual: bfloat16 [512, 64, 4096], P('dp', None, 'tensor'), may hold values from -128 to 128
- queries: bfloat16 [512, 64, 4096], P('dp', None, 'tensor'), may hold values from -30 to 30
- attn_keys: bfloat16 [512, 64, 512], P('dp', None, 'tensor'), may hold values from -6 to 6
- values: bfloat16 [512, 64, 512], P('dp', None, 'tensor'), may hold values from -6 to 6
- out_weight: bfloat16 [4096, 4096], P('tensor'), may hold values from -0.09375 to 0.09375
- norm_gain: float32 [4096], P('tensor'), may hold values from 0.1 to 1.9
- probe_weight: float32 [4096, 64], P('tensor'), may hold values from -0.09375 to 0.09375
- partner_slot: int32 [512], P('dp'), may hold values from 0 to 7, as said below
- patch_list: int32 [512, 64, 2], P('dp', 'tensor'), may hold values from 0 to 63, as said below
- concept_labels: int32 [512, 64], P('dp'), may hold values from 0 to 63
Outputs:
- attn_out: bfloat16 [512, 64, 4096], P('dp', None, 'tensor')
- logits: float32 [512, 64, 64], P('dp')
- probe_grad: float32 [4096, 64], P('tensor')
The draws below stay inside these ranges and needn't reach their ends.
Inputs may be any that keep to these rules, and one draw needn't show every extreme that they name: Prompt j of device i of dp, for i below 32, is paired with prompt partner_slot of it on device i + 32, and that prompt's partner_slot is j; on each device the values are a permutation. `patch_list`: each entry is (head, position). A prompt's list equals its partner's, entry for entry. Its entries are distinct, and entries k * 16 to (k + 1) * 16 - 1 name heads of the k-th block of 8 consecutive heads.
All inputs are finite; a program needn't handle non-finite values.
Results may differ from the reference program's by a relative error of at most 0.01.
Values may be sent and summed in bfloat16 or wider, within the bound.
No kernel may reach another device: no remote copies, remote signals or barrier semaphores. Data moves between devices by JAX's collectives and lax.ppermute only.
A program may use at most 128 MiB of HBM per device.

```python
import math
import jax
import jax.numpy as jnp
from jax import lax

DW = 4096
HEADS = 32
KV = 4
HDIM = 128
LEN = 64
CONCEPTS = 64
KQ = 16
PROMPTS_DEV = 8
PROMPTS = 512
N_DP = 64
N_TENSOR = 4


def pairing(key):
    half_way = N_DP // 2
    base_key = jax.random.fold_in(key, 101)
    perms = jax.vmap(lambda index: jax.random.permutation(jax.random.fold_in(base_key, index), PROMPTS_DEV))(jnp.arange(half_way))
    perms = perms.astype(jnp.int32)
    counting = jnp.arange(PROMPTS_DEV, dtype=jnp.int32)
    inverse = jax.vmap(lambda order: jnp.zeros((PROMPTS_DEV,), jnp.int32).at[order].set(counting))(perms)
    return jnp.concatenate([perms, inverse], axis=0)


def draw_partner_slot(key, part):
    return pairing(key).reshape(PROMPTS).astype(jnp.int32)


def draw_patch_list(key, part):
    slots = pairing(key)
    half_way = N_DP // 2
    counting = jnp.arange(PROMPTS_DEV, dtype=jnp.int32)
    lower_ids = jnp.arange(half_way, dtype=jnp.int32)[:, None] * PROMPTS_DEV + counting[None, :]
    upper_ids = jnp.arange(half_way, dtype=jnp.int32)[:, None] * PROMPTS_DEV + slots[half_way:]
    pair_ids = jnp.concatenate([lower_ids, upper_ids], axis=0).reshape(PROMPTS)
    block_heads = HEADS // N_TENSOR
    base_key = jax.random.fold_in(key, 202)

    def entries(pair_index, block_index):
        order = jax.random.permutation(jax.random.fold_in(base_key, pair_index * N_TENSOR + block_index), block_heads * LEN)[:KQ]
        order = order.astype(jnp.int32)
        return jnp.stack([block_index * block_heads + order // LEN, order % LEN], axis=-1)
    blocks = jnp.arange(N_TENSOR, dtype=jnp.int32)
    table = jax.vmap(lambda pair_index: jax.vmap(lambda block_index: entries(pair_index, block_index))(blocks))(jnp.arange(half_way * PROMPTS_DEV, dtype=jnp.int32))
    return table[pair_ids].reshape(PROMPTS, N_TENSOR * KQ, 2).astype(jnp.int32)


def attention_pair(key):
    query_key = jax.random.fold_in(key, 301)
    key_key = jax.random.fold_in(key, 302)
    key_rows = jnp.clip(jax.random.normal(key_key, (PROMPTS, LEN, KV * HDIM), jnp.float32), -6.0, 6.0)
    query_rows = 2.0 * jnp.clip(jax.random.normal(query_key, (PROMPTS, LEN, HEADS * HDIM), jnp.float32), -6.0, 6.0)
    return (query_rows, key_rows)


def draw_queries(key, part):
    return attention_pair(key)[0].astype(jnp.bfloat16)


def draw_attn_keys(key, part):
    return attention_pair(key)[1].astype(jnp.bfloat16)


def draw_residual(key, part):
    noise_key = jax.random.fold_in(key, 401)
    row_key = jax.random.fold_in(key, 402)
    column_key = jax.random.fold_in(key, 403)
    shape = (PROMPTS, LEN, DW)
    column_log = jnp.arange(DW).astype(jnp.float32) / DW + jax.random.uniform(column_key, (DW,), jnp.float32, -0.15, 0.15)
    row_log = jax.random.uniform(row_key, (PROMPTS, LEN, 1), jnp.float32, 0.0, 1.0)
    noise = jnp.clip(jax.random.normal(noise_key, shape, jnp.float32), -6.0, 6.0)
    return (0.15 * noise * jnp.power(10.0, row_log) * jnp.power(10.0, column_log)).astype(jnp.bfloat16)


def with_ends(values, stream_key, smallest, largest):
    place = [jax.random.randint(jax.random.fold_in(stream_key, axis), (), 0, length) for axis, length in enumerate(values.shape)]
    longest = values.shape.index(max(values.shape))
    neighbour = place[:longest] + [(place[longest] + 1) % values.shape[longest]] + place[longest + 1:]
    return values.at[tuple(place)].set(smallest).at[tuple(neighbour)].set(largest)


def levels(own_key, extent, split, low, high):
    def one(dim, blocks):
        draws = jax.random.uniform(jax.random.fold_in(jax.random.fold_in(own_key, 6), dim), (blocks,), jnp.float32, low / len(split), high / len(split))
        return jnp.repeat(jnp.exp(draws), extent[dim] // blocks).reshape((-1,) + (1,) * (len(extent) - dim - 1))

    gain = one(*split[0])
    for cut in split[1:]:
        gain = gain * one(*cut)
    return gain


def centred(stream_key, dims, scale, limit, split=(), kind=jnp.bfloat16):
    drawn = scale * jax.random.normal(stream_key, dims, jnp.float32)
    if split:
        drawn = drawn * levels(stream_key, dims, split, -0.22, 0.18)
    return jnp.clip(drawn, -limit, limit).astype(kind)


def setup_inputs(seed: int = 0) -> dict:
    arg_keys = jax.random.split(jax.random.key(seed), 11)
    return {
        "residual": draw_residual(jax.random.fold_in(arg_keys[10], 71), 0),
        "queries": draw_queries(jax.random.fold_in(arg_keys[10], 71), 0),
        "attn_keys": draw_attn_keys(jax.random.fold_in(arg_keys[10], 71), 0),
        "values": centred(arg_keys[3], (PROMPTS, LEN, KV * HDIM), 1.0, 6.0, ((0, 64), (2, 4))),
        "out_weight": centred(arg_keys[4], (HEADS * HDIM, DW), (HEADS * HDIM) ** -0.5, 0.09375, ((0, 4),)),
        "norm_gain": jnp.clip(1.0 + 0.18 * jax.random.normal(arg_keys[5], (DW,), jnp.float32), 0.1, 1.9),
        "probe_weight": centred(arg_keys[6], (DW, CONCEPTS), DW ** -0.5, 0.09375, ((0, 4),), jnp.float32),
        "partner_slot": draw_partner_slot(jax.random.fold_in(arg_keys[10], 71), 0),
        "patch_list": draw_patch_list(jax.random.fold_in(arg_keys[10], 71), 0),
        "concept_labels": with_ends(jax.random.randint(arg_keys[9], (PROMPTS, LEN), 0, CONCEPTS), jax.random.fold_in(arg_keys[9], 1), 0, CONCEPTS - 1).astype(jnp.int32),
    }


norm_epsilon = 1e-05

def attend(queries, attn_keys, values):
    prompt_count = queries.shape[0]
    group_size = HEADS // KV
    query_blocks = queries.astype(jnp.float32).reshape(prompt_count, LEN, KV, group_size, HDIM)
    key_blocks = attn_keys.astype(jnp.float32).reshape(prompt_count, LEN, KV, HDIM)
    value_blocks = values.astype(jnp.float32).reshape(prompt_count, LEN, KV, HDIM)
    scores = jnp.einsum('pqkgd,pskd->pkgqs', query_blocks, key_blocks) / math.sqrt(HDIM)
    causal = jnp.arange(LEN)[:, None] >= jnp.arange(LEN)[None, :]
    scores = jnp.where(causal, scores, -jnp.inf)
    highest = lax.optimization_barrier(jnp.max(scores, axis=-1, keepdims=True))
    exponent = jnp.exp(scores - highest)
    weights = (exponent / lax.optimization_barrier(jnp.sum(exponent, axis=-1, keepdims=True))).astype(jnp.bfloat16)
    weights = lax.optimization_barrier(weights).astype(jnp.float32)
    mixed_rows = jnp.einsum('pkgqs,pskd->pqkgd', weights, value_blocks)
    return mixed_rows.reshape(prompt_count, LEN, HEADS, HDIM).astype(jnp.bfloat16)

def reference(residual, queries, attn_keys, values, out_weight, norm_gain, probe_weight, partner_slot, patch_list, concept_labels):
    heads_out = attend(queries, attn_keys, values)
    half_way = N_DP // 2
    prompt_ids = jnp.arange(PROMPTS, dtype=jnp.int32)
    partner_ids = ((prompt_ids // PROMPTS_DEV + half_way) % N_DP * PROMPTS_DEV + partner_slot).astype(jnp.int32)
    from_partner = heads_out[partner_ids]
    row_ids = jnp.broadcast_to(prompt_ids[:, None], patch_list.shape[:2])
    patch_mask = jnp.zeros((PROMPTS, LEN, HEADS), dtype=bool).at[row_ids, patch_list[..., 1], patch_list[..., 0]].set(True)
    patched = jnp.where(patch_mask[..., None], from_partner, heads_out)
    token_count = PROMPTS * LEN
    flat_heads = patched.reshape(token_count, HEADS * HDIM)
    block_rows = HEADS * HDIM // N_TENSOR
    total = jnp.zeros((token_count, DW), jnp.float32)
    for block_index in range(N_TENSOR):
        lower = block_index * block_rows
        partial_value = jnp.dot(flat_heads[:, lower:lower + block_rows], out_weight[lower:lower + block_rows], preferred_element_type=jnp.float32)
        partial_value = lax.optimization_barrier(partial_value.astype(jnp.bfloat16)).astype(jnp.float32)
        total = total + partial_value
    attn_out = total.astype(jnp.bfloat16)
    hidden = residual.reshape(token_count, DW).astype(jnp.float32) + attn_out.astype(jnp.float32)
    mean_square = lax.optimization_barrier(jnp.sum(hidden * hidden, axis=1, keepdims=True)) / DW
    normed = hidden * lax.rsqrt(mean_square + norm_epsilon) * norm_gain.astype(jnp.float32)
    logits = jnp.dot(normed, probe_weight, precision=lax.Precision.HIGHEST, preferred_element_type=jnp.float32)
    classes = jnp.arange(CONCEPTS, dtype=jnp.int32)
    target = (concept_labels.reshape(token_count)[:, None] == classes[None, :]).astype(jnp.float32)
    error = jax.nn.sigmoid(logits) - target
    probe_grad = jnp.dot(normed.T, error, precision=lax.Precision.HIGHEST, preferred_element_type=jnp.float32) / math.sqrt(token_count)
    return (attn_out.reshape(PROMPTS, LEN, DW), logits.reshape(PROMPTS, LEN, CONCEPTS), probe_grad)
```

```python
import math

import jax
import jax.numpy as jnp
from jax import lax
from jax.sharding import PartitionSpec as P

DW = 4096
HDIM = 128


norm_epsilon = 1e-05


def exchanged(block, axis, bit):
    count = lax.axis_size(axis)
    return lax.ppermute(block, axis, [(i, i ^ bit) for i in range(count)])


def butterfly_sum(block, axis, bits):
    for bit in bits:
        block = block + exchanged(block, axis, bit)
    return block


def tree_all_reduce(block, axis, halving_bits, doubling_bits):
    position = lax.axis_index(axis)
    kept = []
    for bit in halving_bits:
        half = block.shape[0] // 2
        upper = (position // bit) % 2 == 1
        low, high = block[:half], block[half:]
        mine = jnp.where(upper, high, low)
        other = jnp.where(upper, low, high)
        block = mine + exchanged(other, axis, bit)
        kept.append((bit, upper))
    block = butterfly_sum(block, axis, doubling_bits)
    for bit, upper in reversed(kept):
        other = exchanged(block, axis, bit)
        block = jnp.where(upper, jnp.concatenate([other, block]), jnp.concatenate([block, other]))
    return block


def dp_bits(count):
    low = [1 << k for k in range(count.bit_length() - 1)]
    if count == 64:
        return low[:3], low[3:]
    return [], low


def attend(queries, attn_keys, values):
    prompt_count = queries.shape[0]
    seq_length = queries.shape[1]
    local_kv = attn_keys.shape[2] // HDIM
    local_heads = queries.shape[2] // HDIM
    group_size = local_heads // local_kv
    query_blocks = queries.reshape(prompt_count, seq_length, local_kv, group_size, HDIM)
    key_blocks = attn_keys.reshape(prompt_count, seq_length, local_kv, HDIM)
    value_blocks = values.reshape(prompt_count, seq_length, local_kv, HDIM)
    scores = jnp.einsum(
        "pqkgd,pskd->pkgqs", query_blocks, key_blocks, preferred_element_type=jnp.float32
    ) / math.sqrt(HDIM)
    causal = jnp.arange(seq_length)[:, None] >= jnp.arange(seq_length)[None, :]
    scores = jnp.where(causal, scores, -jnp.inf)
    highest = jnp.max(scores, axis=-1, keepdims=True)
    exponent = jnp.exp(scores - highest)
    weights = (exponent / jnp.sum(exponent, axis=-1, keepdims=True)).astype(jnp.bfloat16)
    mixed_rows = jnp.einsum(
        "pkgqs,pskd->pqkgd", weights, value_blocks, preferred_element_type=jnp.float32
    )
    return mixed_rows.astype(jnp.bfloat16).reshape(prompt_count, seq_length, local_heads, HDIM)


def per_device(
    residual,
    queries,
    attn_keys,
    values,
    out_weight,
    norm_gain,
    probe_weight,
    partner_slot,
    patch_list,
    concept_labels,
):
    prompt_count = residual.shape[0]
    seq_length = residual.shape[1]
    feature_count = residual.shape[2]
    token_count = prompt_count * seq_length
    heads_out = attend(queries, attn_keys, values)
    local_heads = heads_out.shape[2]
    rows = seq_length * local_heads
    flat_heads = heads_out.reshape(prompt_count, rows, HDIM)

    entry_rows = patch_list[..., 1] * local_heads + patch_list[..., 0] % local_heads
    picks = entry_rows[:, :, None] == jnp.arange(rows, dtype=jnp.int32)[None, None, :]
    pick_values = picks.astype(jnp.bfloat16)
    own_entries = jnp.einsum(
        "jkr,jrd->jkd", pick_values, flat_heads, preferred_element_type=jnp.float32
    ).astype(jnp.bfloat16)

    half_way = lax.axis_size("dp") // 2
    arrived = exchanged(own_entries, "dp", half_way)
    slot_pick = (
        partner_slot[:, None] == jnp.arange(prompt_count, dtype=partner_slot.dtype)[None, :]
    ).astype(jnp.bfloat16)
    incoming = jnp.einsum(
        "jm,mkd->jkd", slot_pick, arrived, preferred_element_type=jnp.float32
    ).astype(jnp.bfloat16)
    placed = jnp.einsum(
        "jkr,jkd->jrd", pick_values, incoming, preferred_element_type=jnp.float32
    ).astype(jnp.bfloat16)
    patch_mask = jnp.any(picks, axis=1)
    patched = jnp.where(patch_mask[..., None], placed, flat_heads)

    partial_value = jnp.dot(
        patched.reshape(token_count, -1), out_weight, preferred_element_type=jnp.float32
    )
    attn_local = lax.psum_scatter(
        partial_value.astype(jnp.bfloat16), "tensor", scatter_dimension=1, tiled=True
    )
    hidden = residual.reshape(token_count, feature_count).astype(jnp.float32) + attn_local.astype(
        jnp.float32
    )
    square_local = jnp.sum(hidden * hidden, axis=1)
    scaled = hidden * norm_gain
    raw_part = jnp.dot(
        scaled, probe_weight, precision=lax.Precision.HIGHEST, preferred_element_type=jnp.float32
    )
    concepts = probe_weight.shape[1]
    packed = jnp.concatenate([raw_part, square_local[:, None]], axis=1)
    tensor_count = lax.axis_size("tensor")
    packed = butterfly_sum(packed, "tensor", [1 << k for k in range(tensor_count.bit_length() - 1)])
    raw_logits = packed[:, :concepts]
    square_sum = packed[:, concepts]
    inverse_rms = lax.rsqrt(square_sum / DW + norm_epsilon)
    logits = raw_logits * inverse_rms[:, None]
    normed = scaled * inverse_rms[:, None]
    classes = jnp.arange(concepts, dtype=jnp.int32)
    target = (concept_labels.reshape(token_count)[:, None] == classes[None, :]).astype(jnp.float32)
    error = jax.nn.sigmoid(logits) - target
    total_tokens = token_count * lax.axis_size("dp")
    grad_local = lax.dot_general(
        normed,
        error,
        (((0,), (0,)), ((), ())),
        precision=lax.Precision.HIGHEST,
        preferred_element_type=jnp.float32,
    ) / math.sqrt(total_tokens)
    halving_bits, doubling_bits = dp_bits(lax.axis_size("dp"))
    probe_grad = tree_all_reduce(grad_local, "dp", halving_bits, doubling_bits)
    return (
        attn_local.reshape(prompt_count, seq_length, feature_count),
        logits.reshape(prompt_count, seq_length, -1),
        probe_grad,
    )


def solution(mesh):
    return jax.shard_map(
        per_device,
        mesh=mesh,
        in_specs=(
            P("dp", None, "tensor"),
            P("dp", None, "tensor"),
            P("dp", None, "tensor"),
            P("dp", None, "tensor"),
            P("tensor", None),
            P("tensor"),
            P("tensor", None),
            P("dp"),
            P("dp", "tensor", None),
            P("dp", None),
        ),
        out_specs=(P("dp", None, "tensor"), P("dp", None, None), P("tensor", None)),
        check_vma=False,
    )
```

```python
import math

import jax
import jax.numpy as jnp
from jax import lax
from jax.sharding import PartitionSpec as P

DW = 4096
HDIM = 128


norm_epsilon = 1e-05


def exchanged(block, axis, bit):
    count = lax.axis_size(axis)
    return lax.ppermute(block, axis, [(i, i ^ bit) for i in range(count)])


def butterfly_sum(block, axis, bits):
    for bit in bits:
        block = block + exchanged(block, axis, bit)
    return block


def tree_all_reduce(block, axis, halving_bits, doubling_bits):
    position = lax.axis_index(axis)
    kept = []
    for bit in halving_bits:
        half = block.shape[0] // 2
        upper = (position // bit) % 2 == 1
        low, high = block[:half], block[half:]
        mine = jnp.where(upper, high, low)
        other = jnp.where(upper, low, high)
        block = mine + exchanged(other, axis, bit)
        kept.append((bit, upper))
    block = butterfly_sum(block, axis, doubling_bits)
    for bit, upper in reversed(kept):
        other = exchanged(block, axis, bit)
        block = jnp.where(upper, jnp.concatenate([other, block]), jnp.concatenate([block, other]))
    return block


def block_reduce_scatter(partial, axis):
    count = lax.axis_size(axis)
    position = lax.axis_index(axis)
    blocks = partial.reshape(partial.shape[0], count, partial.shape[1] // count)

    def block(index):
        return lax.dynamic_index_in_dim(blocks, index, 1, keepdims=False)

    if count != 4:
        total = block(position)
        for bit in range(1, count):
            total = total + exchanged(block(position ^ bit).astype(jnp.bfloat16), axis, bit).astype(jnp.float32)
        return total
    far = position ^ 2
    far_sum = block(far) + exchanged(block(far ^ 1).astype(jnp.bfloat16), axis, 1).astype(jnp.float32)
    from_far = exchanged(far_sum.astype(jnp.bfloat16), axis, 2)
    near = exchanged(block(position ^ 1).astype(jnp.bfloat16), axis, 1)
    return block(position) + near.astype(jnp.float32) + from_far.astype(jnp.float32)


def dp_bits(count):
    low = [1 << k for k in range(count.bit_length() - 1)]
    if count == 64:
        return low[:3], low[3:]
    return [], low


def attend(queries, attn_keys, values):
    prompt_count = queries.shape[0]
    seq_length = queries.shape[1]
    local_kv = attn_keys.shape[2] // HDIM
    local_heads = queries.shape[2] // HDIM
    group_size = local_heads // local_kv
    query_blocks = queries.reshape(prompt_count, seq_length, local_kv, group_size, HDIM)
    key_blocks = attn_keys.reshape(prompt_count, seq_length, local_kv, HDIM)
    value_blocks = values.reshape(prompt_count, seq_length, local_kv, HDIM)
    scores = jnp.einsum(
        "pqkgd,pskd->pkgqs", query_blocks, key_blocks, preferred_element_type=jnp.float32
    ) / math.sqrt(HDIM)
    causal = jnp.arange(seq_length)[:, None] >= jnp.arange(seq_length)[None, :]
    scores = jnp.where(causal, scores, -jnp.inf)
    highest = jnp.max(scores, axis=-1, keepdims=True)
    exponent = jnp.exp(scores - highest)
    weights = (exponent / jnp.sum(exponent, axis=-1, keepdims=True)).astype(jnp.bfloat16)
    mixed_rows = jnp.einsum(
        "pkgqs,pskd->pqkgd", weights, value_blocks, preferred_element_type=jnp.float32
    )
    return mixed_rows.astype(jnp.bfloat16).reshape(prompt_count, seq_length, local_heads, HDIM)


def per_device(
    residual,
    queries,
    attn_keys,
    values,
    out_weight,
    norm_gain,
    probe_weight,
    partner_slot,
    patch_list,
    concept_labels,
):
    prompt_count = residual.shape[0]
    seq_length = residual.shape[1]
    feature_count = residual.shape[2]
    token_count = prompt_count * seq_length
    heads_out = attend(queries, attn_keys, values)
    local_heads = heads_out.shape[2]
    rows = seq_length * local_heads
    flat_heads = heads_out.reshape(prompt_count, rows, HDIM)

    entry_rows = patch_list[..., 1] * local_heads + patch_list[..., 0] % local_heads
    picks = entry_rows[:, :, None] == jnp.arange(rows, dtype=jnp.int32)[None, None, :]
    pick_values = picks.astype(jnp.bfloat16)
    own_entries = jnp.einsum(
        "jkr,jrd->jkd", pick_values, flat_heads, preferred_element_type=jnp.float32
    ).astype(jnp.bfloat16)

    half_way = lax.axis_size("dp") // 2
    arrived = exchanged(own_entries, "dp", half_way)
    slot_pick = (
        partner_slot[:, None] == jnp.arange(prompt_count, dtype=partner_slot.dtype)[None, :]
    ).astype(jnp.bfloat16)
    incoming = jnp.einsum(
        "jm,mkd->jkd", slot_pick, arrived, preferred_element_type=jnp.float32
    ).astype(jnp.bfloat16)
    placed = jnp.einsum(
        "jkr,jkd->jrd", pick_values, incoming, preferred_element_type=jnp.float32
    ).astype(jnp.bfloat16)
    patch_mask = jnp.any(picks, axis=1)
    patched = jnp.where(patch_mask[..., None], placed, flat_heads)

    partial_value = jnp.dot(
        patched.reshape(token_count, -1), out_weight, preferred_element_type=jnp.float32
    )
    attn_local = block_reduce_scatter(partial_value, "tensor").astype(jnp.bfloat16)
    hidden = residual.reshape(token_count, feature_count).astype(jnp.float32) + attn_local.astype(
        jnp.float32
    )
    square_local = jnp.sum(hidden * hidden, axis=1)
    scaled = hidden * norm_gain
    raw_part = jnp.dot(
        scaled, probe_weight, precision=lax.Precision.HIGHEST, preferred_element_type=jnp.float32
    )
    concepts = probe_weight.shape[1]
    packed = jnp.concatenate([raw_part, square_local[:, None]], axis=1)
    tensor_count = lax.axis_size("tensor")
    packed = butterfly_sum(packed, "tensor", [1 << k for k in range(tensor_count.bit_length() - 1)])
    raw_logits = packed[:, :concepts]
    square_sum = packed[:, concepts]
    inverse_rms = lax.rsqrt(square_sum / DW + norm_epsilon)
    logits = raw_logits * inverse_rms[:, None]
    normed = scaled * inverse_rms[:, None]
    classes = jnp.arange(concepts, dtype=jnp.int32)
    target = (concept_labels.reshape(token_count)[:, None] == classes[None, :]).astype(jnp.float32)
    error = jax.nn.sigmoid(logits) - target
    total_tokens = token_count * lax.axis_size("dp")
    grad_local = lax.dot_general(
        normed,
        error,
        (((0,), (0,)), ((), ())),
        precision=lax.Precision.HIGHEST,
        preferred_element_type=jnp.float32,
    ) / math.sqrt(total_tokens)
    halving_bits, doubling_bits = dp_bits(lax.axis_size("dp"))
    probe_grad = tree_all_reduce(grad_local, "dp", halving_bits, doubling_bits)
    return (
        attn_local.reshape(prompt_count, seq_length, feature_count),
        logits.reshape(prompt_count, seq_length, -1),
        probe_grad,
    )


def solution(mesh):
    return jax.shard_map(
        per_device,
        mesh=mesh,
        in_specs=(
            P("dp", None, "tensor"),
            P("dp", None, "tensor"),
            P("dp", None, "tensor"),
            P("dp", None, "tensor"),
            P("tensor", None),
            P("tensor"),
            P("tensor", None),
            P("dp"),
            P("dp", "tensor", None),
            P("dp", None),
        ),
        out_specs=(P("dp", None, "tensor"), P("dp", None, None), P("tensor", None)),
        check_vma=False,
    )
```

```python
import math

import jax
import jax.numpy as jnp
from jax import lax
from jax.sharding import PartitionSpec as P

DW = 4096
HDIM = 128


norm_epsilon = 1e-05


def exchanged(block, axis, bit):
    count = lax.axis_size(axis)
    return lax.ppermute(block, axis, [(i, i ^ bit) for i in range(count)])


def butterfly_sum(block, axis, bits):
    for bit in bits:
        block = block + exchanged(block, axis, bit)
    return block


def tree_all_reduce(block, axis, halving_bits, doubling_bits):
    position = lax.axis_index(axis)
    kept = []
    for bit in halving_bits:
        half = block.shape[0] // 2
        upper = (position // bit) % 2 == 1
        low, high = block[:half], block[half:]
        mine = jnp.where(upper, high, low)
        other = jnp.where(upper, low, high)
        block = mine + exchanged(other, axis, bit)
        kept.append((bit, upper))
    block = butterfly_sum(block, axis, doubling_bits)
    for bit, upper in reversed(kept):
        other = exchanged(block, axis, bit)
        block = jnp.where(upper, jnp.concatenate([other, block]), jnp.concatenate([block, other]))
    return block


def block_reduce_scatter(heads, weight, axis):
    count = lax.axis_size(axis)
    position = lax.axis_index(axis)
    width = weight.shape[1] // count

    def block(index):
        columns = lax.dynamic_slice_in_dim(weight, index * width, width, axis=1)
        return jnp.dot(heads, columns, preferred_element_type=jnp.float32)

    def sent(value, bit):
        return exchanged(value.astype(jnp.bfloat16), axis, bit).astype(jnp.float32)

    if count != 4:
        total = block(position)
        for bit in range(1, count):
            total = total + sent(block(position ^ bit), bit)
        return total
    far = position ^ 2
    from_partner = sent(block(far ^ 1), 1)
    from_far = sent(block(far) + from_partner, 2)
    near = sent(block(position ^ 1), 1)
    return block(position) + near + from_far


def dp_bits(count):
    low = [1 << k for k in range(count.bit_length() - 1)]
    if count == 64:
        return low[:2], low[2:]
    return [], low


def attend(queries, attn_keys, values):
    prompt_count = queries.shape[0]
    seq_length = queries.shape[1]
    local_kv = attn_keys.shape[2] // HDIM
    local_heads = queries.shape[2] // HDIM
    group_size = local_heads // local_kv
    query_blocks = queries.reshape(prompt_count, seq_length, local_kv, group_size, HDIM)
    key_blocks = attn_keys.reshape(prompt_count, seq_length, local_kv, HDIM)
    value_blocks = values.reshape(prompt_count, seq_length, local_kv, HDIM)
    scores = jnp.einsum(
        "pqkgd,pskd->pkgqs", query_blocks, key_blocks, preferred_element_type=jnp.float32
    ) / math.sqrt(HDIM)
    causal = jnp.arange(seq_length)[:, None] >= jnp.arange(seq_length)[None, :]
    scores = jnp.where(causal, scores, -jnp.inf)
    highest = jnp.max(scores, axis=-1, keepdims=True)
    exponent = jnp.exp(scores - highest)
    weights = (exponent / jnp.sum(exponent, axis=-1, keepdims=True)).astype(jnp.bfloat16)
    mixed_rows = jnp.einsum(
        "pkgqs,pskd->pqkgd", weights, value_blocks, preferred_element_type=jnp.float32
    )
    return mixed_rows.astype(jnp.bfloat16).reshape(prompt_count, seq_length, local_heads, HDIM)


def per_device(
    residual,
    queries,
    attn_keys,
    values,
    out_weight,
    norm_gain,
    probe_weight,
    partner_slot,
    patch_list,
    concept_labels,
):
    prompt_count = residual.shape[0]
    seq_length = residual.shape[1]
    feature_count = residual.shape[2]
    token_count = prompt_count * seq_length
    heads_out = attend(queries, attn_keys, values)
    local_heads = heads_out.shape[2]
    rows = seq_length * local_heads
    flat_heads = heads_out.reshape(prompt_count, rows, HDIM)

    entry_rows = patch_list[..., 1] * local_heads + patch_list[..., 0] % local_heads
    picks = entry_rows[:, :, None] == jnp.arange(rows, dtype=jnp.int32)[None, None, :]
    pick_values = picks.astype(jnp.bfloat16)
    own_entries = jnp.einsum(
        "jkr,jrd->jkd", pick_values, flat_heads, preferred_element_type=jnp.float32
    ).astype(jnp.bfloat16)

    half_way = lax.axis_size("dp") // 2
    arrived = exchanged(own_entries, "dp", half_way)
    slot_pick = (
        partner_slot[:, None] == jnp.arange(prompt_count, dtype=partner_slot.dtype)[None, :]
    ).astype(jnp.bfloat16)
    incoming = jnp.einsum(
        "jm,mkd->jkd", slot_pick, arrived, preferred_element_type=jnp.float32
    ).astype(jnp.bfloat16)
    placed = jnp.einsum(
        "jkr,jkd->jrd", pick_values, incoming, preferred_element_type=jnp.float32
    ).astype(jnp.bfloat16)
    patch_mask = jnp.any(picks, axis=1)
    patched = jnp.where(patch_mask[..., None], placed, flat_heads)

    attn_local = block_reduce_scatter(
        patched.reshape(token_count, -1), out_weight, "tensor"
    ).astype(jnp.bfloat16)
    hidden = residual.reshape(token_count, feature_count).astype(jnp.float32) + attn_local.astype(
        jnp.float32
    )
    square_local = jnp.sum(hidden * hidden, axis=1)
    scaled = hidden * norm_gain
    raw_part = jnp.dot(
        scaled, probe_weight, precision=lax.Precision.HIGHEST, preferred_element_type=jnp.float32
    )
    concepts = probe_weight.shape[1]
    packed = jnp.concatenate([raw_part, square_local[:, None]], axis=1)
    tensor_count = lax.axis_size("tensor")
    packed = butterfly_sum(packed, "tensor", [1 << k for k in range(tensor_count.bit_length() - 1)])
    raw_logits = packed[:, :concepts]
    square_sum = packed[:, concepts]
    inverse_rms = lax.rsqrt(square_sum / DW + norm_epsilon)
    logits = raw_logits * inverse_rms[:, None]
    normed = scaled * inverse_rms[:, None]
    classes = jnp.arange(concepts, dtype=jnp.int32)
    target = (concept_labels.reshape(token_count)[:, None] == classes[None, :]).astype(jnp.float32)
    error = jax.nn.sigmoid(logits) - target
    total_tokens = token_count * lax.axis_size("dp")
    grad_local = lax.dot_general(
        normed,
        error,
        (((0,), (0,)), ((), ())),
        precision=lax.Precision.HIGHEST,
        preferred_element_type=jnp.float32,
    ) / math.sqrt(total_tokens)
    halving_bits, doubling_bits = dp_bits(lax.axis_size("dp"))
    probe_grad = tree_all_reduce(grad_local, "dp", halving_bits, doubling_bits)
    return (
        attn_local.reshape(prompt_count, seq_length, feature_count),
        logits.reshape(prompt_count, seq_length, -1),
        probe_grad,
    )


def solution(mesh):
    return jax.shard_map(
        per_device,
        mesh=mesh,
        in_specs=(
            P("dp", None, "tensor"),
            P("dp", None, "tensor"),
            P("dp", None, "tensor"),
            P("dp", None, "tensor"),
            P("tensor", None),
            P("tensor"),
            P("tensor", None),
            P("dp"),
            P("dp", "tensor", None),
            P("dp", None),
        ),
        out_specs=(P("dp", None, "tensor"), P("dp", None, None), P("tensor", None)),
        check_vma=False,
    )
```

```python
import math

import jax
import jax.numpy as jnp
from jax import lax
from jax.sharding import PartitionSpec as P

DW = 4096
HDIM = 128


norm_epsilon = 1e-05


def exchanged(block, axis, bit):
    count = lax.axis_size(axis)
    return lax.ppermute(block, axis, [(i, i ^ bit) for i in range(count)])


def butterfly_sum(block, axis, bits):
    for bit in bits:
        block = block + exchanged(block, axis, bit)
    return block


def tree_all_reduce(block, axis, halving_bits, doubling_bits):
    position = lax.axis_index(axis)
    kept = []
    for bit in halving_bits:
        half = block.shape[0] // 2
        upper = (position // bit) % 2 == 1
        low, high = block[:half], block[half:]
        mine = jnp.where(upper, high, low)
        other = jnp.where(upper, low, high)
        block = mine + exchanged(other, axis, bit)
        kept.append((bit, upper))
    block = butterfly_sum(block, axis, doubling_bits)
    for bit, upper in reversed(kept):
        other = exchanged(block, axis, bit)
        block = jnp.where(upper, jnp.concatenate([other, block]), jnp.concatenate([block, other]))
    return block


def block_reduce_scatter(heads, weight, axis):
    count = lax.axis_size(axis)
    position = lax.axis_index(axis)
    width = weight.shape[1] // count

    def block(index):
        columns = lax.dynamic_slice_in_dim(weight, index * width, width, axis=1)
        return jnp.dot(heads, columns, preferred_element_type=jnp.float32)

    def sent(value, bit):
        return exchanged(value.astype(jnp.bfloat16), axis, bit).astype(jnp.float32)

    if count != 4:
        total = block(position)
        for bit in range(1, count):
            total = total + sent(block(position ^ bit), bit)
        return total
    far = position ^ 2
    from_partner = sent(block(far ^ 1), 1)
    far_sum = (block(far) + from_partner).astype(jnp.bfloat16)
    heads, far_sum = lax.optimization_barrier((heads, far_sum))
    from_far = exchanged(far_sum, axis, 2).astype(jnp.float32)
    near = sent(block(position ^ 1), 1)
    return block(position) + near + from_far


def dp_bits(count):
    low = [1 << k for k in range(count.bit_length() - 1)]
    if count == 64:
        return low[:2], low[2:]
    return [], low


def attend(queries, attn_keys, values):
    prompt_count = queries.shape[0]
    seq_length = queries.shape[1]
    local_kv = attn_keys.shape[2] // HDIM
    local_heads = queries.shape[2] // HDIM
    group_size = local_heads // local_kv
    query_blocks = queries.reshape(prompt_count, seq_length, local_kv, group_size, HDIM)
    key_blocks = attn_keys.reshape(prompt_count, seq_length, local_kv, HDIM)
    value_blocks = values.reshape(prompt_count, seq_length, local_kv, HDIM)
    scores = jnp.einsum(
        "pqkgd,pskd->pkgqs", query_blocks, key_blocks, preferred_element_type=jnp.float32
    ) / math.sqrt(HDIM)
    causal = jnp.arange(seq_length)[:, None] >= jnp.arange(seq_length)[None, :]
    scores = jnp.where(causal, scores, -jnp.inf)
    highest = jnp.max(scores, axis=-1, keepdims=True)
    exponent = jnp.exp(scores - highest)
    weights = (exponent / jnp.sum(exponent, axis=-1, keepdims=True)).astype(jnp.bfloat16)
    mixed_rows = jnp.einsum(
        "pkgqs,pskd->pqkgd", weights, value_blocks, preferred_element_type=jnp.float32
    )
    return mixed_rows.astype(jnp.bfloat16).reshape(prompt_count, seq_length, local_heads, HDIM)


def per_device(
    residual,
    queries,
    attn_keys,
    values,
    out_weight,
    norm_gain,
    probe_weight,
    partner_slot,
    patch_list,
    concept_labels,
):
    prompt_count = residual.shape[0]
    seq_length = residual.shape[1]
    feature_count = residual.shape[2]
    token_count = prompt_count * seq_length
    heads_out = attend(queries, attn_keys, values)
    local_heads = heads_out.shape[2]
    rows = seq_length * local_heads
    flat_heads = heads_out.reshape(prompt_count, rows, HDIM)

    entry_rows = patch_list[..., 1] * local_heads + patch_list[..., 0] % local_heads
    picks = entry_rows[:, :, None] == jnp.arange(rows, dtype=jnp.int32)[None, None, :]
    pick_values = picks.astype(jnp.bfloat16)
    own_entries = jnp.einsum(
        "jkr,jrd->jkd", pick_values, flat_heads, preferred_element_type=jnp.float32
    ).astype(jnp.bfloat16)

    half_way = lax.axis_size("dp") // 2
    arrived = exchanged(own_entries, "dp", half_way)
    slot_pick = (
        partner_slot[:, None] == jnp.arange(prompt_count, dtype=partner_slot.dtype)[None, :]
    ).astype(jnp.bfloat16)
    incoming = jnp.einsum(
        "jm,mkd->jkd", slot_pick, arrived, preferred_element_type=jnp.float32
    ).astype(jnp.bfloat16)
    placed = jnp.einsum(
        "jkr,jkd->jrd", pick_values, incoming, preferred_element_type=jnp.float32
    ).astype(jnp.bfloat16)
    patch_mask = jnp.any(picks, axis=1)
    patched = jnp.where(patch_mask[..., None], placed, flat_heads)

    flat_patched = patched.reshape(token_count, -1)
    flat_residual = residual.reshape(token_count, feature_count)
    labels = concept_labels.reshape(token_count)
    concepts = probe_weight.shape[1]
    tensor_bits = [1 << k for k in range(lax.axis_size("tensor").bit_length() - 1)]
    chunk_count = 2 if token_count % 2 == 0 else 1
    chunk = token_count // chunk_count
    attn_chunks, logit_chunks, grad_local = [], [], None
    for index in range(chunk_count):
        rows_here = slice(index * chunk, (index + 1) * chunk)
        attn_local = block_reduce_scatter(flat_patched[rows_here], out_weight, "tensor").astype(
            jnp.bfloat16
        )
        hidden = flat_residual[rows_here].astype(jnp.float32) + attn_local.astype(jnp.float32)
        square_local = jnp.sum(hidden * hidden, axis=1)
        scaled = hidden * norm_gain
        raw_part = jnp.dot(
            scaled, probe_weight, precision=lax.Precision.HIGHEST, preferred_element_type=jnp.float32
        )
        packed = jnp.concatenate([raw_part, square_local[:, None]], axis=1)
        packed = butterfly_sum(packed, "tensor", tensor_bits)
        inverse_rms = lax.rsqrt(packed[:, concepts] / DW + norm_epsilon)
        logits = packed[:, :concepts] * inverse_rms[:, None]
        normed = scaled * inverse_rms[:, None]
        classes = jnp.arange(concepts, dtype=jnp.int32)
        target = (labels[rows_here][:, None] == classes[None, :]).astype(jnp.float32)
        error = jax.nn.sigmoid(logits) - target
        grad_part = lax.dot_general(
            normed,
            error,
            (((0,), (0,)), ((), ())),
            precision=lax.Precision.HIGHEST,
            preferred_element_type=jnp.float32,
        )
        grad_local = grad_part if grad_local is None else grad_local + grad_part
        attn_chunks.append(attn_local)
        logit_chunks.append(logits)
    attn_local = jnp.concatenate(attn_chunks, axis=0)
    logits = jnp.concatenate(logit_chunks, axis=0)
    total_tokens = token_count * lax.axis_size("dp")
    grad_local = grad_local / math.sqrt(total_tokens)
    halving_bits, doubling_bits = dp_bits(lax.axis_size("dp"))
    probe_grad = tree_all_reduce(grad_local, "dp", halving_bits, doubling_bits)
    return (
        attn_local.reshape(prompt_count, seq_length, feature_count),
        logits.reshape(prompt_count, seq_length, -1),
        probe_grad,
    )


def solution(mesh):
    return jax.shard_map(
        per_device,
        mesh=mesh,
        in_specs=(
            P("dp", None, "tensor"),
            P("dp", None, "tensor"),
            P("dp", None, "tensor"),
            P("dp", None, "tensor"),
            P("tensor", None),
            P("tensor"),
            P("tensor", None),
            P("dp"),
            P("dp", "tensor", None),
            P("dp", None),
        ),
        out_specs=(P("dp", None, "tensor"), P("dp", None, None), P("tensor", None)),
        check_vma=False,
    )
```

```python
import math

import jax
import jax.numpy as jnp
from jax import lax
from jax.sharding import PartitionSpec as P

DW = 4096
HDIM = 128


norm_epsilon = 1e-05


def exchanged(block, axis, bit):
    count = lax.axis_size(axis)
    return lax.ppermute(block, axis, [(i, i ^ bit) for i in range(count)])


def butterfly_sum(block, axis, bits):
    for bit in bits:
        block = block + exchanged(block, axis, bit)
    return block


def tree_all_reduce(block, axis, halving_bits, doubling_bits):
    position = lax.axis_index(axis)
    kept = []
    for bit in halving_bits:
        half = block.shape[0] // 2
        upper = (position // bit) % 2 == 1
        low, high = block[:half], block[half:]
        mine = jnp.where(upper, high, low)
        other = jnp.where(upper, low, high)
        block = mine + exchanged(other, axis, bit)
        kept.append((bit, upper))
    block = butterfly_sum(block, axis, doubling_bits)
    for bit, upper in reversed(kept):
        other = exchanged(block, axis, bit)
        block = jnp.where(upper, jnp.concatenate([other, block]), jnp.concatenate([block, other]))
    return block


def block_reduce_scatter(heads, weight, axis):
    count = lax.axis_size(axis)
    position = lax.axis_index(axis)
    width = weight.shape[1] // count
    product = jnp.dot(heads, weight, preferred_element_type=jnp.float32)

    def block(index):
        return lax.dynamic_slice_in_dim(product, index * width, width, axis=1)

    def sent(value, bit):
        return exchanged(value.astype(jnp.bfloat16), axis, bit).astype(jnp.float32)

    if count != 4:
        total = block(position)
        for bit in range(1, count):
            total = total + sent(block(position ^ bit), bit)
        return total
    far = position ^ 2
    from_partner = sent(block(far ^ 1), 1)
    far_sum = (block(far) + from_partner).astype(jnp.bfloat16)
    from_far = exchanged(far_sum, axis, 2).astype(jnp.float32)
    near = sent(block(position ^ 1), 1)
    return block(position) + near + from_far


def dp_bits(count):
    low = [1 << k for k in range(count.bit_length() - 1)]
    if count == 64:
        return low[:2], low[2:]
    return [], low


def attend(queries, attn_keys, values):
    prompt_count = queries.shape[0]
    seq_length = queries.shape[1]
    local_kv = attn_keys.shape[2] // HDIM
    local_heads = queries.shape[2] // HDIM
    group_size = local_heads // local_kv
    query_blocks = queries.reshape(prompt_count, seq_length, local_kv, group_size, HDIM)
    key_blocks = attn_keys.reshape(prompt_count, seq_length, local_kv, HDIM)
    value_blocks = values.reshape(prompt_count, seq_length, local_kv, HDIM)
    scores = jnp.einsum(
        "pqkgd,pskd->pkgqs", query_blocks, key_blocks, preferred_element_type=jnp.float32
    ) / math.sqrt(HDIM)
    causal = jnp.arange(seq_length)[:, None] >= jnp.arange(seq_length)[None, :]
    scores = jnp.where(causal, scores, -jnp.inf)
    highest = jnp.max(scores, axis=-1, keepdims=True)
    exponent = jnp.exp(scores - highest)
    weights = (exponent / jnp.sum(exponent, axis=-1, keepdims=True)).astype(jnp.bfloat16)
    mixed_rows = jnp.einsum(
        "pkgqs,pskd->pqkgd", weights, value_blocks, preferred_element_type=jnp.float32
    )
    return mixed_rows.astype(jnp.bfloat16).reshape(prompt_count, seq_length, local_heads, HDIM)


def per_device(
    residual,
    queries,
    attn_keys,
    values,
    out_weight,
    norm_gain,
    probe_weight,
    partner_slot,
    patch_list,
    concept_labels,
):
    prompt_count = residual.shape[0]
    seq_length = residual.shape[1]
    feature_count = residual.shape[2]
    token_count = prompt_count * seq_length
    heads_out = attend(queries, attn_keys, values)
    local_heads = heads_out.shape[2]
    rows = seq_length * local_heads
    flat_heads = heads_out.reshape(prompt_count, rows, HDIM)

    entry_rows = patch_list[..., 1] * local_heads + patch_list[..., 0] % local_heads
    picks = entry_rows[:, :, None] == jnp.arange(rows, dtype=jnp.int32)[None, None, :]
    pick_values = picks.astype(jnp.bfloat16)
    own_entries = jnp.einsum(
        "jkr,jrd->jkd", pick_values, flat_heads, preferred_element_type=jnp.float32
    ).astype(jnp.bfloat16)

    half_way = lax.axis_size("dp") // 2
    arrived = exchanged(own_entries, "dp", half_way)
    slot_pick = (
        partner_slot[:, None] == jnp.arange(prompt_count, dtype=partner_slot.dtype)[None, :]
    ).astype(jnp.bfloat16)
    incoming = jnp.einsum(
        "jm,mkd->jkd", slot_pick, arrived, preferred_element_type=jnp.float32
    ).astype(jnp.bfloat16)
    placed = jnp.einsum(
        "jkr,jkd->jrd", pick_values, incoming, preferred_element_type=jnp.float32
    ).astype(jnp.bfloat16)
    patch_mask = jnp.any(picks, axis=1)
    patched = jnp.where(patch_mask[..., None], placed, flat_heads)

    flat_patched = patched.reshape(token_count, -1)
    flat_residual = residual.reshape(token_count, feature_count)
    labels = concept_labels.reshape(token_count)
    concepts = probe_weight.shape[1]
    tensor_bits = [1 << k for k in range(lax.axis_size("tensor").bit_length() - 1)]
    chunk_count = 2 if token_count % 2 == 0 else 1
    chunk = token_count // chunk_count
    attn_chunks, logit_chunks, grad_local = [], [], None
    for index in range(chunk_count):
        rows_here = slice(index * chunk, (index + 1) * chunk)
        attn_local = block_reduce_scatter(flat_patched[rows_here], out_weight, "tensor").astype(
            jnp.bfloat16
        )
        hidden = flat_residual[rows_here].astype(jnp.float32) + attn_local.astype(jnp.float32)
        square_local = jnp.sum(hidden * hidden, axis=1)
        scaled = hidden * norm_gain
        raw_part = jnp.dot(
            scaled, probe_weight, precision=lax.Precision.HIGHEST, preferred_element_type=jnp.float32
        )
        packed = jnp.concatenate([raw_part, square_local[:, None]], axis=1)
        packed = butterfly_sum(packed, "tensor", tensor_bits)
        inverse_rms = lax.rsqrt(packed[:, concepts] / DW + norm_epsilon)
        logits = packed[:, :concepts] * inverse_rms[:, None]
        normed = scaled * inverse_rms[:, None]
        classes = jnp.arange(concepts, dtype=jnp.int32)
        target = (labels[rows_here][:, None] == classes[None, :]).astype(jnp.float32)
        error = jax.nn.sigmoid(logits) - target
        grad_part = lax.dot_general(
            normed,
            error,
            (((0,), (0,)), ((), ())),
            precision=lax.Precision.HIGHEST,
            preferred_element_type=jnp.float32,
        )
        grad_local = grad_part if grad_local is None else grad_local + grad_part
        attn_chunks.append(attn_local)
        logit_chunks.append(logits)
    attn_local = jnp.concatenate(attn_chunks, axis=0)
    logits = jnp.concatenate(logit_chunks, axis=0)
    total_tokens = token_count * lax.axis_size("dp")
    grad_local = grad_local / math.sqrt(total_tokens)
    halving_bits, doubling_bits = dp_bits(lax.axis_size("dp"))
    probe_grad = tree_all_reduce(grad_local, "dp", halving_bits, doubling_bits)
    return (
        attn_local.reshape(prompt_count, seq_length, feature_count),
        logits.reshape(prompt_count, seq_length, -1),
        probe_grad,
    )


def solution(mesh):
    return jax.shard_map(
        per_device,
        mesh=mesh,
        in_specs=(
            P("dp", None, "tensor"),
            P("dp", None, "tensor"),
            P("dp", None, "tensor"),
            P("dp", None, "tensor"),
            P("tensor", None),
            P("tensor"),
            P("tensor", None),
            P("dp"),
            P("dp", "tensor", None),
            P("dp", None),
        ),
        out_specs=(P("dp", None, "tensor"), P("dp", None, None), P("tensor", None)),
        check_vma=False,
    )
```

```python
import math

import jax
import jax.numpy as jnp
from jax import lax
from jax.sharding import PartitionSpec as P

DW = 4096
HDIM = 128


norm_epsilon = 1e-05


def exchanged(block, axis, bit):
    count = lax.axis_size(axis)
    return lax.ppermute(block, axis, [(i, i ^ bit) for i in range(count)])


def butterfly_sum(block, axis, bits):
    for bit in bits:
        block = block + exchanged(block, axis, bit)
    return block


def tree_all_reduce(block, axis, halving_bits, doubling_bits):
    position = lax.axis_index(axis)
    kept = []
    for bit in halving_bits:
        half = block.shape[0] // 2
        upper = (position // bit) % 2 == 1
        low, high = block[:half], block[half:]
        mine = jnp.where(upper, high, low)
        other = jnp.where(upper, low, high)
        block = mine + exchanged(other, axis, bit)
        kept.append((bit, upper))
    block = butterfly_sum(block, axis, doubling_bits)
    for bit, upper in reversed(kept):
        other = exchanged(block, axis, bit)
        block = jnp.where(upper, jnp.concatenate([other, block]), jnp.concatenate([block, other]))
    return block


def far_half(heads, weight, axis, after=None):
    count = lax.axis_size(axis)
    position = lax.axis_index(axis)
    width = weight.shape[1] // count
    if after is not None:
        heads, _ = lax.optimization_barrier((heads, after))

    def block(index):
        columns = lax.dynamic_slice_in_dim(weight, index * width, width, axis=1)
        return jnp.dot(heads, columns, preferred_element_type=jnp.float32)

    def sent(value, bit):
        return exchanged(value.astype(jnp.bfloat16), axis, bit).astype(jnp.float32)

    far = position ^ 2
    from_partner = sent(block(far ^ 1), 1)
    far_sum = (block(far) + from_partner).astype(jnp.bfloat16)
    heads, far_sum = lax.optimization_barrier((heads, far_sum))
    return heads, far_sum, exchanged(far_sum, axis, 2)


def near_half(heads, weight, axis, from_far):
    count = lax.axis_size(axis)
    position = lax.axis_index(axis)
    width = weight.shape[1] // count

    def block(index):
        columns = lax.dynamic_slice_in_dim(weight, index * width, width, axis=1)
        return jnp.dot(heads, columns, preferred_element_type=jnp.float32)

    near = exchanged(block(position ^ 1).astype(jnp.bfloat16), axis, 1).astype(jnp.float32)
    return block(position) + near + from_far.astype(jnp.float32)


def dp_bits(count):
    low = [1 << k for k in range(count.bit_length() - 1)]
    if count == 64:
        return low[:2], low[2:]
    return [], low


def attend(queries, attn_keys, values):
    prompt_count = queries.shape[0]
    seq_length = queries.shape[1]
    local_kv = attn_keys.shape[2] // HDIM
    local_heads = queries.shape[2] // HDIM
    group_size = local_heads // local_kv
    query_blocks = queries.reshape(prompt_count, seq_length, local_kv, group_size, HDIM)
    key_blocks = attn_keys.reshape(prompt_count, seq_length, local_kv, HDIM)
    value_blocks = values.reshape(prompt_count, seq_length, local_kv, HDIM)
    scores = jnp.einsum(
        "pqkgd,pskd->pkgqs", query_blocks, key_blocks, preferred_element_type=jnp.float32
    ) / math.sqrt(HDIM)
    causal = jnp.arange(seq_length)[:, None] >= jnp.arange(seq_length)[None, :]
    scores = jnp.where(causal, scores, -jnp.inf)
    highest = jnp.max(scores, axis=-1, keepdims=True)
    exponent = jnp.exp(scores - highest)
    weights = (exponent / jnp.sum(exponent, axis=-1, keepdims=True)).astype(jnp.bfloat16)
    mixed_rows = jnp.einsum(
        "pkgqs,pskd->pqkgd", weights, value_blocks, preferred_element_type=jnp.float32
    )
    return mixed_rows.astype(jnp.bfloat16).reshape(prompt_count, seq_length, local_heads, HDIM)


def per_device(
    residual,
    queries,
    attn_keys,
    values,
    out_weight,
    norm_gain,
    probe_weight,
    partner_slot,
    patch_list,
    concept_labels,
):
    prompt_count = residual.shape[0]
    seq_length = residual.shape[1]
    feature_count = residual.shape[2]
    token_count = prompt_count * seq_length
    heads_out = attend(queries, attn_keys, values)
    local_heads = heads_out.shape[2]
    rows = seq_length * local_heads
    flat_heads = heads_out.reshape(prompt_count, rows, HDIM)

    entry_rows = patch_list[..., 1] * local_heads + patch_list[..., 0] % local_heads
    picks = entry_rows[:, :, None] == jnp.arange(rows, dtype=jnp.int32)[None, None, :]
    pick_values = picks.astype(jnp.bfloat16)
    own_entries = jnp.einsum(
        "jkr,jrd->jkd", pick_values, flat_heads, preferred_element_type=jnp.float32
    ).astype(jnp.bfloat16)

    half_way = lax.axis_size("dp") // 2
    arrived = exchanged(own_entries, "dp", half_way)
    slot_pick = (
        partner_slot[:, None] == jnp.arange(prompt_count, dtype=partner_slot.dtype)[None, :]
    ).astype(jnp.bfloat16)
    incoming = jnp.einsum(
        "jm,mkd->jkd", slot_pick, arrived, preferred_element_type=jnp.float32
    ).astype(jnp.bfloat16)
    placed = jnp.einsum(
        "jkr,jkd->jrd", pick_values, incoming, preferred_element_type=jnp.float32
    ).astype(jnp.bfloat16)
    patch_mask = jnp.any(picks, axis=1)
    patched = jnp.where(patch_mask[..., None], placed, flat_heads)

    flat_patched = patched.reshape(token_count, -1)
    flat_residual = residual.reshape(token_count, feature_count)
    labels = concept_labels.reshape(token_count)
    concepts = probe_weight.shape[1]
    tensor_bits = [1 << k for k in range(lax.axis_size("tensor").bit_length() - 1)]
    chunk_count = 2 if token_count % 2 == 0 else 1
    chunk = token_count // chunk_count
    halves, sent_block = [], None
    for index in range(chunk_count):
        rows_here = slice(index * chunk, (index + 1) * chunk)
        heads_here, sent_block, from_far = far_half(
            flat_patched[rows_here], out_weight, "tensor", sent_block
        )
        halves.append((heads_here, sent_block, from_far))
    attn_chunks, logit_chunks, grad_local = [], [], None
    for index in range(chunk_count):
        rows_here = slice(index * chunk, (index + 1) * chunk)
        heads_here, _, from_far = halves[index]
        if index + 1 < chunk_count:
            from_far, _ = lax.optimization_barrier((from_far, halves[index + 1][1]))
        attn_local = near_half(heads_here, out_weight, "tensor", from_far).astype(jnp.bfloat16)
        hidden = flat_residual[rows_here].astype(jnp.float32) + attn_local.astype(jnp.float32)
        square_local = jnp.sum(hidden * hidden, axis=1)
        scaled = hidden * norm_gain
        raw_part = jnp.dot(
            scaled, probe_weight, precision=lax.Precision.HIGHEST, preferred_element_type=jnp.float32
        )
        packed = jnp.concatenate([raw_part, square_local[:, None]], axis=1)
        packed = butterfly_sum(packed, "tensor", tensor_bits)
        inverse_rms = lax.rsqrt(packed[:, concepts] / DW + norm_epsilon)
        logits = packed[:, :concepts] * inverse_rms[:, None]
        normed = scaled * inverse_rms[:, None]
        classes = jnp.arange(concepts, dtype=jnp.int32)
        target = (labels[rows_here][:, None] == classes[None, :]).astype(jnp.float32)
        error = jax.nn.sigmoid(logits) - target
        grad_part = lax.dot_general(
            normed,
            error,
            (((0,), (0,)), ((), ())),
            precision=lax.Precision.HIGHEST,
            preferred_element_type=jnp.float32,
        )
        grad_local = grad_part if grad_local is None else grad_local + grad_part
        attn_chunks.append(attn_local)
        logit_chunks.append(logits)
    attn_local = jnp.concatenate(attn_chunks, axis=0)
    logits = jnp.concatenate(logit_chunks, axis=0)
    total_tokens = token_count * lax.axis_size("dp")
    grad_local = grad_local / math.sqrt(total_tokens)
    halving_bits, doubling_bits = dp_bits(lax.axis_size("dp"))
    probe_grad = tree_all_reduce(grad_local, "dp", halving_bits, doubling_bits)
    return (
        attn_local.reshape(prompt_count, seq_length, feature_count),
        logits.reshape(prompt_count, seq_length, -1),
        probe_grad,
    )


def solution(mesh):
    return jax.shard_map(
        per_device,
        mesh=mesh,
        in_specs=(
            P("dp", None, "tensor"),
            P("dp", None, "tensor"),
            P("dp", None, "tensor"),
            P("dp", None, "tensor"),
            P("tensor", None),
            P("tensor"),
            P("tensor", None),
            P("dp"),
            P("dp", "tensor", None),
            P("dp", None),
        ),
        out_specs=(P("dp", None, "tensor"), P("dp", None, None), P("tensor", None)),
        check_vma=False,
    )
```

```python
import math

import jax
import jax.numpy as jnp
from jax import lax
from jax.sharding import PartitionSpec as P

DW = 4096
HDIM = 128


norm_epsilon = 1e-05


def exchanged(block, axis, bit):
    count = lax.axis_size(axis)
    return lax.ppermute(block, axis, [(i, i ^ bit) for i in range(count)])


def butterfly_sum(block, axis, bits):
    for bit in bits:
        block = block + exchanged(block, axis, bit)
    return block


def tree_all_reduce(block, axis, halving_bits, doubling_bits):
    position = lax.axis_index(axis)
    kept = []
    for bit in halving_bits:
        half = block.shape[0] // 2
        upper = (position // bit) % 2 == 1
        low, high = block[:half], block[half:]
        mine = jnp.where(upper, high, low)
        other = jnp.where(upper, low, high)
        block = mine + exchanged(other, axis, bit)
        kept.append((bit, upper))
    block = butterfly_sum(block, axis, doubling_bits)
    for bit, upper in reversed(kept):
        other = exchanged(block, axis, bit)
        block = jnp.where(upper, jnp.concatenate([other, block]), jnp.concatenate([block, other]))
    return block


def far_half(heads, weight, axis, after=None):
    count = lax.axis_size(axis)
    position = lax.axis_index(axis)
    width = weight.shape[1] // count
    if after is not None:
        heads, _ = lax.optimization_barrier((heads, after))

    def block(index):
        columns = lax.dynamic_slice_in_dim(weight, index * width, width, axis=1)
        return jnp.dot(heads, columns, preferred_element_type=jnp.float32)

    def sent(value, bit):
        return exchanged(value.astype(jnp.bfloat16), axis, bit).astype(jnp.float32)

    far = position ^ 2
    from_partner = sent(block(far ^ 1), 1)
    far_sum = (block(far) + from_partner).astype(jnp.bfloat16)
    heads, far_sum = lax.optimization_barrier((heads, far_sum))
    return heads, far_sum, exchanged(far_sum, axis, 2)


def near_half(heads, weight, axis, from_far):
    count = lax.axis_size(axis)
    position = lax.axis_index(axis)
    width = weight.shape[1] // count

    def block(index):
        columns = lax.dynamic_slice_in_dim(weight, index * width, width, axis=1)
        return jnp.dot(heads, columns, preferred_element_type=jnp.float32)

    near = exchanged(block(position ^ 1).astype(jnp.bfloat16), axis, 1).astype(jnp.float32)
    return block(position) + near + from_far.astype(jnp.float32)


def dp_bits(count):
    low = [1 << k for k in range(count.bit_length() - 1)]
    if count == 64:
        return low[:2], low[2:]
    return [], low


def attend(queries, attn_keys, values):
    prompt_count = queries.shape[0]
    seq_length = queries.shape[1]
    local_kv = attn_keys.shape[2] // HDIM
    local_heads = queries.shape[2] // HDIM
    group_size = local_heads // local_kv
    query_blocks = queries.reshape(prompt_count, seq_length, local_kv, group_size, HDIM)
    key_blocks = attn_keys.reshape(prompt_count, seq_length, local_kv, HDIM)
    value_blocks = values.reshape(prompt_count, seq_length, local_kv, HDIM)
    scores = jnp.einsum(
        "pqkgd,pskd->pkgqs", query_blocks, key_blocks, preferred_element_type=jnp.float32
    ) / math.sqrt(HDIM)
    causal = jnp.arange(seq_length)[:, None] >= jnp.arange(seq_length)[None, :]
    scores = jnp.where(causal, scores, -jnp.inf)
    highest = jnp.max(scores, axis=-1, keepdims=True)
    exponent = jnp.exp(scores - highest)
    weights = (exponent / jnp.sum(exponent, axis=-1, keepdims=True)).astype(jnp.bfloat16)
    mixed_rows = jnp.einsum(
        "pkgqs,pskd->pqkgd", weights, value_blocks, preferred_element_type=jnp.float32
    )
    return mixed_rows.astype(jnp.bfloat16).reshape(prompt_count, seq_length, local_heads, HDIM)


def attend_rows(queries, attn_keys, values, pick_values, head_ids, pos_ids):
    prompt_count = queries.shape[0]
    seq_length = queries.shape[1]
    local_kv = attn_keys.shape[2] // HDIM
    local_heads = queries.shape[2] // HDIM
    group_size = local_heads // local_kv
    query_rows = jnp.einsum(
        "jkr,jrd->jkd",
        pick_values,
        queries.reshape(prompt_count, seq_length * local_heads, HDIM),
        preferred_element_type=jnp.float32,
    ).astype(queries.dtype)
    key_blocks = attn_keys.reshape(prompt_count, seq_length, local_kv, HDIM)
    value_blocks = values.reshape(prompt_count, seq_length, local_kv, HDIM)
    kv_pick = (
        (head_ids // group_size)[:, :, None] == jnp.arange(local_kv, dtype=head_ids.dtype)[None, None, :]
    ).astype(jnp.float32)
    all_scores = jnp.einsum(
        "jkd,jsvd->jksv", query_rows, key_blocks, preferred_element_type=jnp.float32
    )
    scores = jnp.sum(all_scores * kv_pick[:, :, None, :], axis=-1) / math.sqrt(HDIM)
    causal = jnp.arange(seq_length)[None, None, :] <= pos_ids[:, :, None]
    scores = jnp.where(causal, scores, -jnp.inf)
    highest = jnp.max(scores, axis=-1, keepdims=True)
    exponent = jnp.exp(scores - highest)
    weights = (exponent / jnp.sum(exponent, axis=-1, keepdims=True)).astype(jnp.bfloat16)
    all_rows = jnp.einsum(
        "jks,jsvd->jkvd", weights, value_blocks, preferred_element_type=jnp.float32
    )
    mixed = jnp.sum(all_rows * kv_pick[..., None], axis=2)
    return mixed.astype(jnp.bfloat16)


def per_device(
    residual,
    queries,
    attn_keys,
    values,
    out_weight,
    norm_gain,
    probe_weight,
    partner_slot,
    patch_list,
    concept_labels,
):
    prompt_count = residual.shape[0]
    seq_length = residual.shape[1]
    feature_count = residual.shape[2]
    token_count = prompt_count * seq_length
    local_heads = queries.shape[2] // HDIM
    rows = seq_length * local_heads

    entry_rows = patch_list[..., 1] * local_heads + patch_list[..., 0] % local_heads
    picks = entry_rows[:, :, None] == jnp.arange(rows, dtype=jnp.int32)[None, None, :]
    pick_values = picks.astype(jnp.bfloat16)
    own_entries = attend_rows(
        queries, attn_keys, values, pick_values, patch_list[..., 0] % local_heads, patch_list[..., 1]
    )
    heads_out = attend(queries, attn_keys, values)
    flat_heads = heads_out.reshape(prompt_count, rows, HDIM)

    half_way = lax.axis_size("dp") // 2
    arrived = exchanged(own_entries, "dp", half_way)
    slot_pick = (
        partner_slot[:, None] == jnp.arange(prompt_count, dtype=partner_slot.dtype)[None, :]
    ).astype(jnp.bfloat16)
    incoming = jnp.einsum(
        "jm,mkd->jkd", slot_pick, arrived, preferred_element_type=jnp.float32
    ).astype(jnp.bfloat16)
    placed = jnp.einsum(
        "jkr,jkd->jrd", pick_values, incoming, preferred_element_type=jnp.float32
    ).astype(jnp.bfloat16)
    patch_mask = jnp.any(picks, axis=1)
    patched = jnp.where(patch_mask[..., None], placed, flat_heads)

    flat_patched = patched.reshape(token_count, -1)
    flat_residual = residual.reshape(token_count, feature_count)
    labels = concept_labels.reshape(token_count)
    concepts = probe_weight.shape[1]
    tensor_bits = [1 << k for k in range(lax.axis_size("tensor").bit_length() - 1)]
    chunk_count = 2 if token_count % 2 == 0 else 1
    chunk = token_count // chunk_count
    halves, sent_block = [], None
    for index in range(chunk_count):
        rows_here = slice(index * chunk, (index + 1) * chunk)
        heads_here, sent_block, from_far = far_half(
            flat_patched[rows_here], out_weight, "tensor", sent_block
        )
        halves.append((heads_here, sent_block, from_far))
    attn_chunks, logit_chunks, grad_local = [], [], None
    for index in range(chunk_count):
        rows_here = slice(index * chunk, (index + 1) * chunk)
        heads_here, _, from_far = halves[index]
        if index + 1 < chunk_count:
            from_far, _ = lax.optimization_barrier((from_far, halves[index + 1][1]))
        attn_local = near_half(heads_here, out_weight, "tensor", from_far).astype(jnp.bfloat16)
        hidden = flat_residual[rows_here].astype(jnp.float32) + attn_local.astype(jnp.float32)
        square_local = jnp.sum(hidden * hidden, axis=1)
        scaled = hidden * norm_gain
        raw_part = jnp.dot(
            scaled, probe_weight, precision=lax.Precision.HIGHEST, preferred_element_type=jnp.float32
        )
        packed = jnp.concatenate([raw_part, square_local[:, None]], axis=1)
        packed = butterfly_sum(packed, "tensor", tensor_bits)
        inverse_rms = lax.rsqrt(packed[:, concepts] / DW + norm_epsilon)
        logits = packed[:, :concepts] * inverse_rms[:, None]
        normed = scaled * inverse_rms[:, None]
        classes = jnp.arange(concepts, dtype=jnp.int32)
        target = (labels[rows_here][:, None] == classes[None, :]).astype(jnp.float32)
        error = jax.nn.sigmoid(logits) - target
        grad_part = lax.dot_general(
            normed,
            error,
            (((0,), (0,)), ((), ())),
            precision=lax.Precision.HIGHEST,
            preferred_element_type=jnp.float32,
        )
        grad_local = grad_part if grad_local is None else grad_local + grad_part
        attn_chunks.append(attn_local)
        logit_chunks.append(logits)
    attn_local = jnp.concatenate(attn_chunks, axis=0)
    logits = jnp.concatenate(logit_chunks, axis=0)
    total_tokens = token_count * lax.axis_size("dp")
    grad_local = grad_local / math.sqrt(total_tokens)
    halving_bits, doubling_bits = dp_bits(lax.axis_size("dp"))
    probe_grad = tree_all_reduce(grad_local, "dp", halving_bits, doubling_bits)
    return (
        attn_local.reshape(prompt_count, seq_length, feature_count),
        logits.reshape(prompt_count, seq_length, -1),
        probe_grad,
    )


def solution(mesh):
    return jax.shard_map(
        per_device,
        mesh=mesh,
        in_specs=(
            P("dp", None, "tensor"),
            P("dp", None, "tensor"),
            P("dp", None, "tensor"),
            P("dp", None, "tensor"),
            P("tensor", None),
            P("tensor"),
            P("tensor", None),
            P("dp"),
            P("dp", "tensor", None),
            P("dp", None),
        ),
        out_specs=(P("dp", None, "tensor"), P("dp", None, None), P("tensor", None)),
        check_vma=False,
    )
```

```python
import math

import jax
import jax.numpy as jnp
from jax import lax
from jax.sharding import PartitionSpec as P

DW = 4096
HDIM = 128


norm_epsilon = 1e-05


def exchanged(block, axis, bit):
    count = lax.axis_size(axis)
    return lax.ppermute(block, axis, [(i, i ^ bit) for i in range(count)])


def butterfly_sum(block, axis, bits):
    for bit in bits:
        block = block + exchanged(block, axis, bit)
    return block


def tree_all_reduce(block, axis, halving_bits, doubling_bits):
    position = lax.axis_index(axis)
    kept = []
    for bit in halving_bits:
        half = block.shape[0] // 2
        upper = (position // bit) % 2 == 1
        low, high = block[:half], block[half:]
        mine = jnp.where(upper, high, low)
        other = jnp.where(upper, low, high)
        block = mine + exchanged(other, axis, bit)
        kept.append((bit, upper))
    block = butterfly_sum(block, axis, doubling_bits)
    for bit, upper in reversed(kept):
        other = exchanged(block, axis, bit)
        block = jnp.where(upper, jnp.concatenate([other, block]), jnp.concatenate([block, other]))
    return block


def far_half(heads, weight, axis, after=None):
    count = lax.axis_size(axis)
    position = lax.axis_index(axis)
    width = weight.shape[1] // count
    if after is not None:
        heads, _ = lax.optimization_barrier((heads, after))

    def block(index):
        columns = lax.dynamic_slice_in_dim(weight, index * width, width, axis=1)
        return jnp.dot(heads, columns, preferred_element_type=jnp.float32)

    def sent(value, bit):
        return exchanged(value.astype(jnp.bfloat16), axis, bit).astype(jnp.float32)

    far = position ^ 2
    from_partner = sent(block(far ^ 1), 1)
    far_sum = (block(far) + from_partner).astype(jnp.bfloat16)
    heads, far_sum = lax.optimization_barrier((heads, far_sum))
    return heads, far_sum, exchanged(far_sum, axis, 2)


def near_half(heads, weight, axis, from_far):
    count = lax.axis_size(axis)
    position = lax.axis_index(axis)
    width = weight.shape[1] // count

    def block(index):
        columns = lax.dynamic_slice_in_dim(weight, index * width, width, axis=1)
        return jnp.dot(heads, columns, preferred_element_type=jnp.float32)

    near = exchanged(block(position ^ 1).astype(jnp.bfloat16), axis, 1).astype(jnp.float32)
    return block(position) + near + from_far.astype(jnp.float32)


def dp_bits(count):
    low = [1 << k for k in range(count.bit_length() - 1)]
    if count == 64:
        return low[:2], low[2:]
    return [], low


def attend(queries, attn_keys, values):
    prompt_count = queries.shape[0]
    seq_length = queries.shape[1]
    local_kv = attn_keys.shape[2] // HDIM
    local_heads = queries.shape[2] // HDIM
    group_size = local_heads // local_kv
    query_blocks = queries.reshape(prompt_count, seq_length, local_kv, group_size, HDIM)
    key_blocks = attn_keys.reshape(prompt_count, seq_length, local_kv, HDIM)
    value_blocks = values.reshape(prompt_count, seq_length, local_kv, HDIM)
    scores = jnp.einsum(
        "pqkgd,pskd->pkgqs", query_blocks, key_blocks, preferred_element_type=jnp.float32
    ) / math.sqrt(HDIM)
    causal = jnp.arange(seq_length)[:, None] >= jnp.arange(seq_length)[None, :]
    scores = jnp.where(causal, scores, -jnp.inf)
    highest = jnp.max(scores, axis=-1, keepdims=True)
    exponent = jnp.exp(scores - highest)
    weights = (exponent / jnp.sum(exponent, axis=-1, keepdims=True)).astype(jnp.bfloat16)
    mixed_rows = jnp.einsum(
        "pkgqs,pskd->pqkgd", weights, value_blocks, preferred_element_type=jnp.float32
    )
    return mixed_rows.astype(jnp.bfloat16).reshape(prompt_count, seq_length, local_heads, HDIM)


def attend_rows(queries, attn_keys, values, head_ids, pos_ids):
    prompt_count = queries.shape[0]
    seq_length = queries.shape[1]
    local_kv = attn_keys.shape[2] // HDIM
    local_heads = queries.shape[2] // HDIM
    group_size = local_heads // local_kv
    pos_pick = (
        pos_ids[:, :, None] == jnp.arange(seq_length, dtype=pos_ids.dtype)[None, None, :]
    ).astype(queries.dtype)
    head_pick = (
        head_ids[:, :, None] == jnp.arange(local_heads, dtype=head_ids.dtype)[None, None, :]
    ).astype(queries.dtype)
    query_lines = jnp.einsum(
        "jks,jsf->jkf", pos_pick, queries, preferred_element_type=jnp.float32
    ).astype(queries.dtype)
    query_rows = jnp.einsum(
        "jkh,jkhd->jkd",
        head_pick,
        query_lines.reshape(prompt_count, -1, local_heads, HDIM),
        preferred_element_type=jnp.float32,
    ).astype(queries.dtype)
    key_blocks = attn_keys.reshape(prompt_count, seq_length, local_kv, HDIM)
    value_blocks = values.reshape(prompt_count, seq_length, local_kv, HDIM)
    kv_pick = (
        (head_ids // group_size)[:, :, None] == jnp.arange(local_kv, dtype=head_ids.dtype)[None, None, :]
    ).astype(jnp.float32)
    all_scores = jnp.einsum(
        "jkd,jsvd->jksv", query_rows, key_blocks, preferred_element_type=jnp.float32
    )
    scores = jnp.sum(all_scores * kv_pick[:, :, None, :], axis=-1) / math.sqrt(HDIM)
    causal = jnp.arange(seq_length)[None, None, :] <= pos_ids[:, :, None]
    scores = jnp.where(causal, scores, -jnp.inf)
    highest = jnp.max(scores, axis=-1, keepdims=True)
    exponent = jnp.exp(scores - highest)
    weights = (exponent / jnp.sum(exponent, axis=-1, keepdims=True)).astype(jnp.bfloat16)
    all_rows = jnp.einsum(
        "jks,jsvd->jkvd", weights, value_blocks, preferred_element_type=jnp.float32
    )
    mixed = jnp.sum(all_rows * kv_pick[..., None], axis=2)
    return mixed.astype(jnp.bfloat16)


def per_device(
    residual,
    queries,
    attn_keys,
    values,
    out_weight,
    norm_gain,
    probe_weight,
    partner_slot,
    patch_list,
    concept_labels,
):
    prompt_count = residual.shape[0]
    seq_length = residual.shape[1]
    feature_count = residual.shape[2]
    token_count = prompt_count * seq_length
    local_heads = queries.shape[2] // HDIM
    rows = seq_length * local_heads

    entry_rows = patch_list[..., 1] * local_heads + patch_list[..., 0] % local_heads
    picks = entry_rows[:, :, None] == jnp.arange(rows, dtype=jnp.int32)[None, None, :]
    pick_values = picks.astype(jnp.bfloat16)
    own_entries = attend_rows(
        queries, attn_keys, values, patch_list[..., 0] % local_heads, patch_list[..., 1]
    )
    heads_out = attend(queries, attn_keys, values)
    flat_heads = heads_out.reshape(prompt_count, rows, HDIM)

    half_way = lax.axis_size("dp") // 2
    arrived = exchanged(own_entries, "dp", half_way)
    slot_pick = (
        partner_slot[:, None] == jnp.arange(prompt_count, dtype=partner_slot.dtype)[None, :]
    ).astype(jnp.bfloat16)
    incoming = jnp.einsum(
        "jm,mkd->jkd", slot_pick, arrived, preferred_element_type=jnp.float32
    ).astype(jnp.bfloat16)
    placed = jnp.einsum(
        "jkr,jkd->jrd", pick_values, incoming, preferred_element_type=jnp.float32
    ).astype(jnp.bfloat16)
    patch_mask = jnp.any(picks, axis=1)
    patched = jnp.where(patch_mask[..., None], placed, flat_heads)

    flat_patched = patched.reshape(token_count, -1)
    flat_residual = residual.reshape(token_count, feature_count)
    labels = concept_labels.reshape(token_count)
    concepts = probe_weight.shape[1]
    tensor_bits = [1 << k for k in range(lax.axis_size("tensor").bit_length() - 1)]
    chunk_count = 2 if token_count % 2 == 0 else 1
    chunk = token_count // chunk_count
    halves, sent_block = [], None
    for index in range(chunk_count):
        rows_here = slice(index * chunk, (index + 1) * chunk)
        heads_here, sent_block, from_far = far_half(
            flat_patched[rows_here], out_weight, "tensor", sent_block
        )
        halves.append((heads_here, sent_block, from_far))
    attn_chunks, logit_chunks, grad_local = [], [], None
    for index in range(chunk_count):
        rows_here = slice(index * chunk, (index + 1) * chunk)
        heads_here, _, from_far = halves[index]
        if index + 1 < chunk_count:
            from_far, _ = lax.optimization_barrier((from_far, halves[index + 1][1]))
        attn_local = near_half(heads_here, out_weight, "tensor", from_far).astype(jnp.bfloat16)
        hidden = flat_residual[rows_here].astype(jnp.float32) + attn_local.astype(jnp.float32)
        square_local = jnp.sum(hidden * hidden, axis=1)
        scaled = hidden * norm_gain
        raw_part = jnp.dot(
            scaled, probe_weight, precision=lax.Precision.HIGHEST, preferred_element_type=jnp.float32
        )
        packed = jnp.concatenate([raw_part, square_local[:, None]], axis=1)
        packed = butterfly_sum(packed, "tensor", tensor_bits)
        inverse_rms = lax.rsqrt(packed[:, concepts] / DW + norm_epsilon)
        logits = packed[:, :concepts] * inverse_rms[:, None]
        normed = scaled * inverse_rms[:, None]
        classes = jnp.arange(concepts, dtype=jnp.int32)
        target = (labels[rows_here][:, None] == classes[None, :]).astype(jnp.float32)
        error = jax.nn.sigmoid(logits) - target
        grad_part = lax.dot_general(
            normed,
            error,
            (((0,), (0,)), ((), ())),
            precision=lax.Precision.HIGHEST,
            preferred_element_type=jnp.float32,
        )
        grad_local = grad_part if grad_local is None else grad_local + grad_part
        attn_chunks.append(attn_local)
        logit_chunks.append(logits)
    attn_local = jnp.concatenate(attn_chunks, axis=0)
    logits = jnp.concatenate(logit_chunks, axis=0)
    total_tokens = token_count * lax.axis_size("dp")
    grad_local = grad_local / math.sqrt(total_tokens)
    halving_bits, doubling_bits = dp_bits(lax.axis_size("dp"))
    probe_grad = tree_all_reduce(grad_local, "dp", halving_bits, doubling_bits)
    return (
        attn_local.reshape(prompt_count, seq_length, feature_count),
        logits.reshape(prompt_count, seq_length, -1),
        probe_grad,
    )


def solution(mesh):
    return jax.shard_map(
        per_device,
        mesh=mesh,
        in_specs=(
            P("dp", None, "tensor"),
            P("dp", None, "tensor"),
            P("dp", None, "tensor"),
            P("dp", None, "tensor"),
            P("tensor", None),
            P("tensor"),
            P("tensor", None),
            P("dp"),
            P("dp", "tensor", None),
            P("dp", None),
        ),
        out_specs=(P("dp", None, "tensor"), P("dp", None, None), P("tensor", None)),
        check_vma=False,
    )
```

```python
import math

import jax
import jax.numpy as jnp
from jax import lax
from jax.sharding import PartitionSpec as P

DW = 4096
HDIM = 128


norm_epsilon = 1e-05


def exchanged(block, axis, bit):
    count = lax.axis_size(axis)
    return lax.ppermute(block, axis, [(i, i ^ bit) for i in range(count)])


def butterfly_sum(block, axis, bits):
    for bit in bits:
        block = block + exchanged(block, axis, bit)
    return block


def tree_all_reduce(block, axis, halving_bits, doubling_bits):
    position = lax.axis_index(axis)
    kept = []
    for bit in halving_bits:
        half = block.shape[0] // 2
        upper = (position // bit) % 2 == 1
        low, high = block[:half], block[half:]
        mine = jnp.where(upper, high, low)
        other = jnp.where(upper, low, high)
        block = mine + exchanged(other, axis, bit)
        kept.append((bit, upper))
    block = butterfly_sum(block, axis, doubling_bits)
    for bit, upper in reversed(kept):
        other = exchanged(block, axis, bit)
        block = jnp.where(upper, jnp.concatenate([other, block]), jnp.concatenate([block, other]))
    return block


def far_half(heads, weight, axis, after=None):
    count = lax.axis_size(axis)
    position = lax.axis_index(axis)
    width = weight.shape[1] // count
    if after is not None:
        heads, _ = lax.optimization_barrier((heads, after))

    def block(index):
        columns = lax.dynamic_slice_in_dim(weight, index * width, width, axis=1)
        return jnp.dot(heads, columns, preferred_element_type=jnp.float32)

    def sent(value, bit):
        return exchanged(value.astype(jnp.bfloat16), axis, bit).astype(jnp.float32)

    far = position ^ 2
    partner_share = block(far ^ 1).astype(jnp.bfloat16)
    from_partner = exchanged(partner_share, axis, 1).astype(jnp.float32)
    far_sum = (block(far) + from_partner).astype(jnp.bfloat16)
    heads, far_sum = lax.optimization_barrier((heads, far_sum))
    return heads, partner_share, exchanged(far_sum, axis, 2)


def near_half(heads, weight, axis, from_far):
    count = lax.axis_size(axis)
    position = lax.axis_index(axis)
    width = weight.shape[1] // count

    def block(index):
        columns = lax.dynamic_slice_in_dim(weight, index * width, width, axis=1)
        return jnp.dot(heads, columns, preferred_element_type=jnp.float32)

    near = exchanged(block(position ^ 1).astype(jnp.bfloat16), axis, 1).astype(jnp.float32)
    return block(position) + near + from_far.astype(jnp.float32)


def dp_bits(count):
    low = [1 << k for k in range(count.bit_length() - 1)]
    if count == 64:
        return low[:2], low[2:]
    return [], low


def attend(queries, attn_keys, values):
    prompt_count = queries.shape[0]
    seq_length = queries.shape[1]
    local_kv = attn_keys.shape[2] // HDIM
    local_heads = queries.shape[2] // HDIM
    group_size = local_heads // local_kv
    query_blocks = queries.reshape(prompt_count, seq_length, local_kv, group_size, HDIM)
    key_blocks = attn_keys.reshape(prompt_count, seq_length, local_kv, HDIM)
    value_blocks = values.reshape(prompt_count, seq_length, local_kv, HDIM)
    scores = jnp.einsum(
        "pqkgd,pskd->pkgqs", query_blocks, key_blocks, preferred_element_type=jnp.float32
    ) / math.sqrt(HDIM)
    causal = jnp.arange(seq_length)[:, None] >= jnp.arange(seq_length)[None, :]
    scores = jnp.where(causal, scores, -jnp.inf)
    highest = jnp.max(scores, axis=-1, keepdims=True)
    exponent = jnp.exp(scores - highest)
    weights = (exponent / jnp.sum(exponent, axis=-1, keepdims=True)).astype(jnp.bfloat16)
    mixed_rows = jnp.einsum(
        "pkgqs,pskd->pqkgd", weights, value_blocks, preferred_element_type=jnp.float32
    )
    return mixed_rows.astype(jnp.bfloat16).reshape(prompt_count, seq_length, local_heads, HDIM)


def attend_rows(queries, attn_keys, values, pick_values, head_ids, pos_ids):
    prompt_count = queries.shape[0]
    seq_length = queries.shape[1]
    local_kv = attn_keys.shape[2] // HDIM
    local_heads = queries.shape[2] // HDIM
    group_size = local_heads // local_kv
    query_rows = jnp.einsum(
        "jkr,jrd->jkd",
        pick_values,
        queries.reshape(prompt_count, seq_length * local_heads, HDIM),
        preferred_element_type=jnp.float32,
    ).astype(queries.dtype)
    key_blocks = attn_keys.reshape(prompt_count, seq_length, local_kv, HDIM)
    value_blocks = values.reshape(prompt_count, seq_length, local_kv, HDIM)
    kv_pick = (
        (head_ids // group_size)[:, :, None] == jnp.arange(local_kv, dtype=head_ids.dtype)[None, None, :]
    ).astype(jnp.float32)
    all_scores = jnp.einsum(
        "jkd,jsvd->jksv", query_rows, key_blocks, preferred_element_type=jnp.float32
    )
    scores = jnp.sum(all_scores * kv_pick[:, :, None, :], axis=-1) / math.sqrt(HDIM)
    causal = jnp.arange(seq_length)[None, None, :] <= pos_ids[:, :, None]
    scores = jnp.where(causal, scores, -jnp.inf)
    highest = jnp.max(scores, axis=-1, keepdims=True)
    exponent = jnp.exp(scores - highest)
    weights = (exponent / jnp.sum(exponent, axis=-1, keepdims=True)).astype(jnp.bfloat16)
    all_rows = jnp.einsum(
        "jks,jsvd->jkvd", weights, value_blocks, preferred_element_type=jnp.float32
    )
    mixed = jnp.sum(all_rows * kv_pick[..., None], axis=2)
    return mixed.astype(jnp.bfloat16)


def per_device(
    residual,
    queries,
    attn_keys,
    values,
    out_weight,
    norm_gain,
    probe_weight,
    partner_slot,
    patch_list,
    concept_labels,
):
    prompt_count = residual.shape[0]
    seq_length = residual.shape[1]
    feature_count = residual.shape[2]
    token_count = prompt_count * seq_length
    local_heads = queries.shape[2] // HDIM
    rows = seq_length * local_heads

    entry_rows = patch_list[..., 1] * local_heads + patch_list[..., 0] % local_heads
    picks = entry_rows[:, :, None] == jnp.arange(rows, dtype=jnp.int32)[None, None, :]
    pick_values = picks.astype(jnp.bfloat16)
    own_entries = attend_rows(
        queries, attn_keys, values, pick_values, patch_list[..., 0] % local_heads, patch_list[..., 1]
    )
    heads_out = attend(queries, attn_keys, values)
    flat_heads = heads_out.reshape(prompt_count, rows, HDIM)

    half_way = lax.axis_size("dp") // 2
    arrived = exchanged(own_entries, "dp", half_way)
    slot_pick = (
        partner_slot[:, None] == jnp.arange(prompt_count, dtype=partner_slot.dtype)[None, :]
    ).astype(jnp.bfloat16)
    incoming = jnp.einsum(
        "jm,mkd->jkd", slot_pick, arrived, preferred_element_type=jnp.float32
    ).astype(jnp.bfloat16)
    placed = jnp.einsum(
        "jkr,jkd->jrd", pick_values, incoming, preferred_element_type=jnp.float32
    ).astype(jnp.bfloat16)
    patch_mask = jnp.any(picks, axis=1)
    patched = jnp.where(patch_mask[..., None], placed, flat_heads)

    flat_patched = patched.reshape(token_count, -1)
    flat_residual = residual.reshape(token_count, feature_count)
    labels = concept_labels.reshape(token_count)
    concepts = probe_weight.shape[1]
    tensor_bits = [1 << k for k in range(lax.axis_size("tensor").bit_length() - 1)]
    chunk_count = 2 if token_count % 2 == 0 else 1
    chunk = token_count // chunk_count
    halves, sent_block = [], None
    for index in range(chunk_count):
        rows_here = slice(index * chunk, (index + 1) * chunk)
        heads_here, sent_block, from_far = far_half(
            flat_patched[rows_here], out_weight, "tensor", sent_block
        )
        halves.append((heads_here, sent_block, from_far))
    attn_chunks, logit_chunks, grad_local = [], [], None
    for index in range(chunk_count):
        rows_here = slice(index * chunk, (index + 1) * chunk)
        heads_here, _, from_far = halves[index]
        if index + 1 < chunk_count:
            from_far, _ = lax.optimization_barrier((from_far, halves[index + 1][1]))
        attn_local = near_half(heads_here, out_weight, "tensor", from_far).astype(jnp.bfloat16)
        hidden = flat_residual[rows_here].astype(jnp.float32) + attn_local.astype(jnp.float32)
        square_local = jnp.sum(hidden * hidden, axis=1)
        scaled = hidden * norm_gain
        raw_part = jnp.dot(
            scaled, probe_weight, precision=lax.Precision.HIGHEST, preferred_element_type=jnp.float32
        )
        packed = jnp.concatenate([raw_part, square_local[:, None]], axis=1)
        packed = butterfly_sum(packed, "tensor", tensor_bits)
        inverse_rms = lax.rsqrt(packed[:, concepts] / DW + norm_epsilon)
        logits = packed[:, :concepts] * inverse_rms[:, None]
        normed = scaled * inverse_rms[:, None]
        classes = jnp.arange(concepts, dtype=jnp.int32)
        target = (labels[rows_here][:, None] == classes[None, :]).astype(jnp.float32)
        error = jax.nn.sigmoid(logits) - target
        grad_part = lax.dot_general(
            normed,
            error,
            (((0,), (0,)), ((), ())),
            precision=lax.Precision.HIGHEST,
            preferred_element_type=jnp.float32,
        )
        grad_local = grad_part if grad_local is None else grad_local + grad_part
        attn_chunks.append(attn_local)
        logit_chunks.append(logits)
    attn_local = jnp.concatenate(attn_chunks, axis=0)
    logits = jnp.concatenate(logit_chunks, axis=0)
    total_tokens = token_count * lax.axis_size("dp")
    grad_local = grad_local / math.sqrt(total_tokens)
    halving_bits, doubling_bits = dp_bits(lax.axis_size("dp"))
    probe_grad = tree_all_reduce(grad_local, "dp", halving_bits, doubling_bits)
    return (
        attn_local.reshape(prompt_count, seq_length, feature_count),
        logits.reshape(prompt_count, seq_length, -1),
        probe_grad,
    )


def solution(mesh):
    return jax.shard_map(
        per_device,
        mesh=mesh,
        in_specs=(
            P("dp", None, "tensor"),
            P("dp", None, "tensor"),
            P("dp", None, "tensor"),
            P("dp", None, "tensor"),
            P("tensor", None),
            P("tensor"),
            P("tensor", None),
            P("dp"),
            P("dp", "tensor", None),
            P("dp", None),
        ),
        out_specs=(P("dp", None, "tensor"), P("dp", None, None), P("tensor", None)),
        check_vma=False,
    )
```

```python
import math

import jax
import jax.numpy as jnp
from jax import lax
from jax.sharding import PartitionSpec as P

DW = 4096
HDIM = 128


norm_epsilon = 1e-05


def exchanged(block, axis, bit):
    count = lax.axis_size(axis)
    return lax.ppermute(block, axis, [(i, i ^ bit) for i in range(count)])


def butterfly_sum(block, axis, bits):
    for bit in bits:
        block = block + exchanged(block, axis, bit)
    return block


def tree_all_reduce(block, axis, halving_bits, doubling_bits):
    position = lax.axis_index(axis)
    kept = []
    for bit in halving_bits:
        half = block.shape[0] // 2
        upper = (position // bit) % 2 == 1
        low, high = block[:half], block[half:]
        mine = jnp.where(upper, high, low)
        other = jnp.where(upper, low, high)
        block = mine + exchanged(other, axis, bit)
        kept.append((bit, upper))
    block = butterfly_sum(block, axis, doubling_bits)
    for bit, upper in reversed(kept):
        other = exchanged(block, axis, bit)
        block = jnp.where(upper, jnp.concatenate([other, block]), jnp.concatenate([block, other]))
    return block


def far_half(heads, weight, axis, after=None):
    count = lax.axis_size(axis)
    position = lax.axis_index(axis)
    width = weight.shape[1] // count
    if after is not None:
        heads, _ = lax.optimization_barrier((heads, after))

    def block(index):
        columns = lax.dynamic_slice_in_dim(weight, index * width, width, axis=1)
        return jnp.dot(heads, columns, preferred_element_type=jnp.float32)

    def sent(value, bit):
        return exchanged(value.astype(jnp.bfloat16), axis, bit).astype(jnp.float32)

    far = position ^ 2
    partner_share = block(far ^ 1).astype(jnp.bfloat16)
    from_partner = exchanged(partner_share, axis, 1).astype(jnp.float32)
    far_sum = (block(far) + from_partner).astype(jnp.bfloat16)
    heads, far_sum = lax.optimization_barrier((heads, far_sum))
    return heads, partner_share, exchanged(far_sum, axis, 2)


def near_half(heads, weight, axis, from_far):
    count = lax.axis_size(axis)
    position = lax.axis_index(axis)
    width = weight.shape[1] // count

    def block(index):
        columns = lax.dynamic_slice_in_dim(weight, index * width, width, axis=1)
        return jnp.dot(heads, columns, preferred_element_type=jnp.float32)

    near = exchanged(block(position ^ 1).astype(jnp.bfloat16), axis, 1).astype(jnp.float32)
    return block(position) + near + from_far.astype(jnp.float32)


def dp_bits(count):
    low = [1 << k for k in range(count.bit_length() - 1)]
    if count == 64:
        return low[:2], low[2:]
    return [], low


def attend(queries, attn_keys, values):
    prompt_count = queries.shape[0]
    seq_length = queries.shape[1]
    local_kv = attn_keys.shape[2] // HDIM
    local_heads = queries.shape[2] // HDIM
    group_size = local_heads // local_kv
    query_blocks = queries.reshape(prompt_count, seq_length, local_kv, group_size, HDIM)
    key_blocks = attn_keys.reshape(prompt_count, seq_length, local_kv, HDIM)
    value_blocks = values.reshape(prompt_count, seq_length, local_kv, HDIM)
    scores = jnp.einsum(
        "pqkgd,pskd->pkgqs", query_blocks, key_blocks, preferred_element_type=jnp.float32
    ) / math.sqrt(HDIM)
    causal = jnp.arange(seq_length)[:, None] >= jnp.arange(seq_length)[None, :]
    scores = jnp.where(causal, scores, -jnp.inf)
    highest = jnp.max(scores, axis=-1, keepdims=True)
    exponent = jnp.exp(scores - highest)
    weights = (exponent / jnp.sum(exponent, axis=-1, keepdims=True)).astype(jnp.bfloat16)
    mixed_rows = jnp.einsum(
        "pkgqs,pskd->pqkgd", weights, value_blocks, preferred_element_type=jnp.float32
    )
    return mixed_rows.astype(jnp.bfloat16).reshape(prompt_count, seq_length, local_heads, HDIM)


def attend_rows(queries, attn_keys, values, pick_values, head_ids, pos_ids):
    prompt_count = queries.shape[0]
    seq_length = queries.shape[1]
    local_kv = attn_keys.shape[2] // HDIM
    local_heads = queries.shape[2] // HDIM
    group_size = local_heads // local_kv
    query_rows = jnp.einsum(
        "jkr,jrd->jkd",
        pick_values,
        queries.reshape(prompt_count, seq_length * local_heads, HDIM),
        preferred_element_type=jnp.float32,
    ).astype(queries.dtype)
    key_blocks = attn_keys.reshape(prompt_count, seq_length, local_kv, HDIM)
    value_blocks = values.reshape(prompt_count, seq_length, local_kv, HDIM)
    kv_pick = (
        (head_ids // group_size)[:, :, None] == jnp.arange(local_kv, dtype=head_ids.dtype)[None, None, :]
    ).astype(jnp.float32)
    all_scores = jnp.einsum(
        "jkd,jsvd->jksv", query_rows, key_blocks, preferred_element_type=jnp.float32
    )
    scores = jnp.sum(all_scores * kv_pick[:, :, None, :], axis=-1) / math.sqrt(HDIM)
    causal = jnp.arange(seq_length)[None, None, :] <= pos_ids[:, :, None]
    scores = jnp.where(causal, scores, -jnp.inf)
    highest = jnp.max(scores, axis=-1, keepdims=True)
    exponent = jnp.exp(scores - highest)
    weights = (exponent / jnp.sum(exponent, axis=-1, keepdims=True)).astype(jnp.bfloat16)
    all_rows = jnp.einsum(
        "jks,jsvd->jkvd", weights, value_blocks, preferred_element_type=jnp.float32
    )
    mixed = jnp.sum(all_rows * kv_pick[..., None], axis=2)
    return mixed.astype(jnp.bfloat16)


def per_device(
    residual,
    queries,
    attn_keys,
    values,
    out_weight,
    norm_gain,
    probe_weight,
    partner_slot,
    patch_list,
    concept_labels,
):
    prompt_count = residual.shape[0]
    seq_length = residual.shape[1]
    feature_count = residual.shape[2]
    token_count = prompt_count * seq_length
    local_heads = queries.shape[2] // HDIM
    rows = seq_length * local_heads

    entry_rows = patch_list[..., 1] * local_heads + patch_list[..., 0] % local_heads
    picks = entry_rows[:, :, None] == jnp.arange(rows, dtype=jnp.int32)[None, None, :]
    pick_values = picks.astype(jnp.bfloat16)
    own_entries = attend_rows(
        queries, attn_keys, values, pick_values, patch_list[..., 0] % local_heads, patch_list[..., 1]
    )
    heads_out = attend(queries, attn_keys, values)
    flat_heads = heads_out.reshape(prompt_count, rows, HDIM)

    half_way = lax.axis_size("dp") // 2
    arrived = exchanged(own_entries, "dp", half_way)
    slot_pick = (
        partner_slot[:, None] == jnp.arange(prompt_count, dtype=partner_slot.dtype)[None, :]
    ).astype(jnp.bfloat16)
    incoming = jnp.einsum(
        "jm,mkd->jkd", slot_pick, arrived, preferred_element_type=jnp.float32
    ).astype(jnp.bfloat16)
    placed = jnp.einsum(
        "jkr,jkd->jrd", pick_values, incoming, preferred_element_type=jnp.float32
    ).astype(jnp.bfloat16)
    patch_mask = jnp.any(picks, axis=1)
    patched = jnp.where(patch_mask[..., None], placed, flat_heads)

    flat_patched = patched.reshape(token_count, -1)
    flat_residual = residual.reshape(token_count, feature_count)
    labels = concept_labels.reshape(token_count)
    concepts = probe_weight.shape[1]
    tensor_bits = [1 << k for k in range(lax.axis_size("tensor").bit_length() - 1)]
    chunk_count = 2 if token_count % 2 == 0 else 1
    chunk = token_count // chunk_count
    halves, sent_block = [], None
    for index in range(chunk_count):
        rows_here = slice(index * chunk, (index + 1) * chunk)
        heads_here, sent_block, from_far = far_half(
            flat_patched[rows_here], out_weight, "tensor", sent_block
        )
        halves.append((heads_here, sent_block, from_far))
    attn_chunks, logit_chunks, grad_local, summed = [], [], None, None
    for index in range(chunk_count):
        rows_here = slice(index * chunk, (index + 1) * chunk)
        heads_here, _, from_far = halves[index]
        if index + 1 < chunk_count:
            from_far, _ = lax.optimization_barrier((from_far, halves[index + 1][1]))
        if summed is not None:
            from_far, _ = lax.optimization_barrier((from_far, summed))
        attn_local = near_half(heads_here, out_weight, "tensor", from_far).astype(jnp.bfloat16)
        hidden = flat_residual[rows_here].astype(jnp.float32) + attn_local.astype(jnp.float32)
        square_local = jnp.sum(hidden * hidden, axis=1)
        scaled = hidden * norm_gain
        raw_part = jnp.dot(
            scaled, probe_weight, precision=lax.Precision.HIGHEST, preferred_element_type=jnp.float32
        )
        packed = jnp.concatenate([raw_part, square_local[:, None]], axis=1)
        packed = butterfly_sum(packed, "tensor", tensor_bits)
        summed = packed
        inverse_rms = lax.rsqrt(packed[:, concepts] / DW + norm_epsilon)
        logits = packed[:, :concepts] * inverse_rms[:, None]
        normed = scaled * inverse_rms[:, None]
        classes = jnp.arange(concepts, dtype=jnp.int32)
        target = (labels[rows_here][:, None] == classes[None, :]).astype(jnp.float32)
        error = jax.nn.sigmoid(logits) - target
        grad_part = lax.dot_general(
            normed,
            error,
            (((0,), (0,)), ((), ())),
            precision=lax.Precision.HIGHEST,
            preferred_element_type=jnp.float32,
        )
        grad_local = grad_part if grad_local is None else grad_local + grad_part
        attn_chunks.append(attn_local)
        logit_chunks.append(logits)
    attn_local = jnp.concatenate(attn_chunks, axis=0)
    logits = jnp.concatenate(logit_chunks, axis=0)
    total_tokens = token_count * lax.axis_size("dp")
    grad_local = grad_local / math.sqrt(total_tokens)
    halving_bits, doubling_bits = dp_bits(lax.axis_size("dp"))
    probe_grad = tree_all_reduce(grad_local, "dp", halving_bits, doubling_bits)
    return (
        attn_local.reshape(prompt_count, seq_length, feature_count),
        logits.reshape(prompt_count, seq_length, -1),
        probe_grad,
    )


def solution(mesh):
    return jax.shard_map(
        per_device,
        mesh=mesh,
        in_specs=(
            P("dp", None, "tensor"),
            P("dp", None, "tensor"),
            P("dp", None, "tensor"),
            P("dp", None, "tensor"),
            P("tensor", None),
            P("tensor"),
            P("tensor", None),
            P("dp"),
            P("dp", "tensor", None),
            P("dp", None),
        ),
        out_specs=(P("dp", None, "tensor"), P("dp", None, None), P("tensor", None)),
        check_vma=False,
    )
```

```python
import math

import jax
import jax.numpy as jnp
from jax import lax
from jax.sharding import PartitionSpec as P

DW = 4096
HDIM = 128


norm_epsilon = 1e-05


def exchanged(block, axis, bit):
    count = lax.axis_size(axis)
    return lax.ppermute(block, axis, [(i, i ^ bit) for i in range(count)])


def butterfly_sum(block, axis, bits):
    for bit in bits:
        block = block + exchanged(block, axis, bit)
    return block


def tree_all_reduce(block, axis, halving_bits, doubling_bits):
    position = lax.axis_index(axis)
    kept = []
    for bit in halving_bits:
        half = block.shape[0] // 2
        upper = (position // bit) % 2 == 1
        low, high = block[:half], block[half:]
        mine = jnp.where(upper, high, low)
        other = jnp.where(upper, low, high)
        block = mine + exchanged(other, axis, bit)
        kept.append((bit, upper))
    block = butterfly_sum(block, axis, doubling_bits)
    for bit, upper in reversed(kept):
        other = exchanged(block, axis, bit)
        block = jnp.where(upper, jnp.concatenate([other, block]), jnp.concatenate([block, other]))
    return block


def far_half(heads, weight, axis, after=None):
    count = lax.axis_size(axis)
    position = lax.axis_index(axis)
    width = weight.shape[1] // count
    if after is not None:
        heads, _ = lax.optimization_barrier((heads, after))

    def block(index):
        columns = lax.dynamic_slice_in_dim(weight, index * width, width, axis=1)
        return jnp.dot(heads, columns, preferred_element_type=jnp.float32)

    def sent(value, bit):
        return exchanged(value.astype(jnp.bfloat16), axis, bit).astype(jnp.float32)

    far = position ^ 2
    partner_share = block(far ^ 1).astype(jnp.bfloat16)
    from_partner = exchanged(partner_share, axis, 1).astype(jnp.float32)
    far_sum = (block(far) + from_partner).astype(jnp.bfloat16)
    heads, far_sum = lax.optimization_barrier((heads, far_sum))
    return heads, partner_share, exchanged(far_sum, axis, 2)


def near_half(heads, weight, axis, from_far):
    count = lax.axis_size(axis)
    position = lax.axis_index(axis)
    width = weight.shape[1] // count

    def block(index):
        columns = lax.dynamic_slice_in_dim(weight, index * width, width, axis=1)
        return jnp.dot(heads, columns, preferred_element_type=jnp.float32)

    near = exchanged(block(position ^ 1).astype(jnp.bfloat16), axis, 1).astype(jnp.float32)
    return block(position) + near + from_far.astype(jnp.float32)


def dp_bits(count):
    low = [1 << k for k in range(count.bit_length() - 1)]
    if count == 64:
        return low[:2], low[2:]
    return [], low


def attend(queries, attn_keys, values):
    prompt_count = queries.shape[0]
    seq_length = queries.shape[1]
    local_kv = attn_keys.shape[2] // HDIM
    local_heads = queries.shape[2] // HDIM
    group_size = local_heads // local_kv
    query_blocks = queries.reshape(prompt_count, seq_length, local_kv, group_size, HDIM)
    key_blocks = attn_keys.reshape(prompt_count, seq_length, local_kv, HDIM)
    value_blocks = values.reshape(prompt_count, seq_length, local_kv, HDIM)
    scores = jnp.einsum(
        "pqkgd,pskd->pkgqs", query_blocks, key_blocks, preferred_element_type=jnp.float32
    ) / math.sqrt(HDIM)
    causal = jnp.arange(seq_length)[:, None] >= jnp.arange(seq_length)[None, :]
    scores = jnp.where(causal, scores, -jnp.inf)
    highest = jnp.max(scores, axis=-1, keepdims=True)
    exponent = jnp.exp(scores - highest)
    weights = (exponent / jnp.sum(exponent, axis=-1, keepdims=True)).astype(jnp.bfloat16)
    mixed_rows = jnp.einsum(
        "pkgqs,pskd->pqkgd", weights, value_blocks, preferred_element_type=jnp.float32
    )
    return mixed_rows.astype(jnp.bfloat16).reshape(prompt_count, seq_length, local_heads, HDIM)


def attend_rows(queries, attn_keys, values, pick_values, head_ids, pos_ids):
    prompt_count = queries.shape[0]
    seq_length = queries.shape[1]
    local_kv = attn_keys.shape[2] // HDIM
    local_heads = queries.shape[2] // HDIM
    group_size = local_heads // local_kv
    query_rows = jnp.einsum(
        "jkr,jrd->jkd",
        pick_values,
        queries.reshape(prompt_count, seq_length * local_heads, HDIM),
        preferred_element_type=jnp.float32,
    ).astype(queries.dtype)
    key_blocks = attn_keys.reshape(prompt_count, seq_length, local_kv, HDIM)
    value_blocks = values.reshape(prompt_count, seq_length, local_kv, HDIM)
    kv_pick = (
        (head_ids // group_size)[:, :, None] == jnp.arange(local_kv, dtype=head_ids.dtype)[None, None, :]
    ).astype(jnp.float32)
    all_scores = jnp.einsum(
        "jkd,jsvd->jksv", query_rows, key_blocks, preferred_element_type=jnp.float32
    )
    scores = jnp.sum(all_scores * kv_pick[:, :, None, :], axis=-1) / math.sqrt(HDIM)
    causal = jnp.arange(seq_length)[None, None, :] <= pos_ids[:, :, None]
    scores = jnp.where(causal, scores, -jnp.inf)
    highest = jnp.max(scores, axis=-1, keepdims=True)
    exponent = jnp.exp(scores - highest)
    weights = (exponent / jnp.sum(exponent, axis=-1, keepdims=True)).astype(jnp.bfloat16)
    all_rows = jnp.einsum(
        "jks,jsvd->jkvd", weights, value_blocks, preferred_element_type=jnp.float32
    )
    mixed = jnp.sum(all_rows * kv_pick[..., None], axis=2)
    return mixed.astype(jnp.bfloat16)


def per_device(
    residual,
    queries,
    attn_keys,
    values,
    out_weight,
    norm_gain,
    probe_weight,
    partner_slot,
    patch_list,
    concept_labels,
):
    prompt_count = residual.shape[0]
    seq_length = residual.shape[1]
    feature_count = residual.shape[2]
    token_count = prompt_count * seq_length
    local_heads = queries.shape[2] // HDIM
    rows = seq_length * local_heads

    entry_rows = patch_list[..., 1] * local_heads + patch_list[..., 0] % local_heads
    picks = entry_rows[:, :, None] == jnp.arange(rows, dtype=jnp.int32)[None, None, :]
    pick_values = picks.astype(jnp.bfloat16)
    own_entries = attend_rows(
        queries, attn_keys, values, pick_values, patch_list[..., 0] % local_heads, patch_list[..., 1]
    )
    heads_out = attend(queries, attn_keys, values)
    flat_heads = heads_out.reshape(prompt_count, rows, HDIM)

    half_way = lax.axis_size("dp") // 2
    arrived = exchanged(own_entries, "dp", half_way)
    slot_pick = (
        partner_slot[:, None] == jnp.arange(prompt_count, dtype=partner_slot.dtype)[None, :]
    ).astype(jnp.bfloat16)
    incoming = jnp.einsum(
        "jm,mkd->jkd", slot_pick, arrived, preferred_element_type=jnp.float32
    ).astype(jnp.bfloat16)
    placed = jnp.einsum(
        "jkr,jkd->jrd", pick_values, incoming, preferred_element_type=jnp.float32
    ).astype(jnp.bfloat16)
    patch_mask = jnp.any(picks, axis=1)
    patched = jnp.where(patch_mask[..., None], placed, flat_heads)

    flat_patched = patched.reshape(token_count, -1)
    flat_residual = residual.reshape(token_count, feature_count)
    labels = concept_labels.reshape(token_count)
    concepts = probe_weight.shape[1]
    tensor_bits = [1 << k for k in range(lax.axis_size("tensor").bit_length() - 1)]
    chunk_count = 2 if token_count % 2 == 0 else 1
    chunk = token_count // chunk_count
    halves, sent_block = [], None
    for index in range(chunk_count):
        rows_here = slice(index * chunk, (index + 1) * chunk)
        heads_here, sent_block, from_far = far_half(
            flat_patched[rows_here], out_weight, "tensor", sent_block
        )
        halves.append((heads_here, sent_block, from_far))
    attn_chunks, logit_chunks, grad_local = [], [], None
    for index in range(chunk_count):
        rows_here = slice(index * chunk, (index + 1) * chunk)
        heads_here, _, from_far = halves[index]
        if index + 1 < chunk_count:
            from_far, _ = lax.optimization_barrier((from_far, halves[index + 1][1]))
        attn_local = near_half(heads_here, out_weight, "tensor", from_far).astype(jnp.bfloat16)
        hidden = flat_residual[rows_here].astype(jnp.float32) + attn_local.astype(jnp.float32)
        square_local = jnp.sum(hidden * hidden, axis=1)
        scaled = hidden * norm_gain
        raw_part = jnp.dot(
            scaled, probe_weight, precision=lax.Precision.HIGH, preferred_element_type=jnp.float32
        )
        packed = jnp.concatenate([raw_part, square_local[:, None]], axis=1)
        packed = butterfly_sum(packed, "tensor", tensor_bits)
        inverse_rms = lax.rsqrt(packed[:, concepts] / DW + norm_epsilon)
        logits = packed[:, :concepts] * inverse_rms[:, None]
        normed = scaled * inverse_rms[:, None]
        classes = jnp.arange(concepts, dtype=jnp.int32)
        target = (labels[rows_here][:, None] == classes[None, :]).astype(jnp.float32)
        error = jax.nn.sigmoid(logits) - target
        grad_part = lax.dot_general(
            normed,
            error,
            (((0,), (0,)), ((), ())),
            precision=lax.Precision.HIGH,
            preferred_element_type=jnp.float32,
        )
        grad_local = grad_part if grad_local is None else grad_local + grad_part
        attn_chunks.append(attn_local)
        logit_chunks.append(logits)
    attn_local = jnp.concatenate(attn_chunks, axis=0)
    logits = jnp.concatenate(logit_chunks, axis=0)
    total_tokens = token_count * lax.axis_size("dp")
    grad_local = grad_local / math.sqrt(total_tokens)
    halving_bits, doubling_bits = dp_bits(lax.axis_size("dp"))
    probe_grad = tree_all_reduce(grad_local, "dp", halving_bits, doubling_bits)
    return (
        attn_local.reshape(prompt_count, seq_length, feature_count),
        logits.reshape(prompt_count, seq_length, -1),
        probe_grad,
    )


def solution(mesh):
    return jax.shard_map(
        per_device,
        mesh=mesh,
        in_specs=(
            P("dp", None, "tensor"),
            P("dp", None, "tensor"),
            P("dp", None, "tensor"),
            P("dp", None, "tensor"),
            P("tensor", None),
            P("tensor"),
            P("tensor", None),
            P("dp"),
            P("dp", "tensor", None),
            P("dp", None),
        ),
        out_specs=(P("dp", None, "tensor"), P("dp", None, None), P("tensor", None)),
        check_vma=False,
    )
```

```python
import math

import jax
import jax.numpy as jnp
from jax import lax
from jax.sharding import PartitionSpec as P

DW = 4096
HDIM = 128


norm_epsilon = 1e-05


def exchanged(block, axis, bit):
    count = lax.axis_size(axis)
    return lax.ppermute(block, axis, [(i, i ^ bit) for i in range(count)])


def butterfly_sum(block, axis, bits):
    for bit in bits:
        block = block + exchanged(block, axis, bit)
    return block


def tree_all_reduce(block, axis, halving_bits, doubling_bits):
    position = lax.axis_index(axis)
    kept = []
    for bit in halving_bits:
        half = block.shape[0] // 2
        upper = (position // bit) % 2 == 1
        low, high = block[:half], block[half:]
        mine = jnp.where(upper, high, low)
        other = jnp.where(upper, low, high)
        block = mine + exchanged(other, axis, bit)
        kept.append((bit, upper))
    block = butterfly_sum(block, axis, doubling_bits)
    for bit, upper in reversed(kept):
        other = exchanged(block, axis, bit)
        block = jnp.where(upper, jnp.concatenate([other, block]), jnp.concatenate([block, other]))
    return block


def far_half(heads, weight, axis, after=None):
    count = lax.axis_size(axis)
    position = lax.axis_index(axis)
    width = weight.shape[1] // count
    if after is not None:
        heads, _ = lax.optimization_barrier((heads, after))

    def block(index):
        columns = lax.dynamic_slice_in_dim(weight, index * width, width, axis=1)
        return jnp.dot(heads, columns, preferred_element_type=jnp.float32)

    def sent(value, bit):
        return exchanged(value.astype(jnp.bfloat16), axis, bit).astype(jnp.float32)

    far = position ^ 2
    partner_share = block(far ^ 1).astype(jnp.bfloat16)
    from_partner = exchanged(partner_share, axis, 1).astype(jnp.float32)
    far_sum = (block(far) + from_partner).astype(jnp.bfloat16)
    heads, far_sum = lax.optimization_barrier((heads, far_sum))
    return heads, partner_share, exchanged(far_sum, axis, 2)


def near_half(heads, weight, axis, from_far):
    count = lax.axis_size(axis)
    position = lax.axis_index(axis)
    width = weight.shape[1] // count

    def block(index):
        columns = lax.dynamic_slice_in_dim(weight, index * width, width, axis=1)
        return jnp.dot(heads, columns, preferred_element_type=jnp.float32)

    near = exchanged(block(position ^ 1).astype(jnp.bfloat16), axis, 1).astype(jnp.float32)
    return block(position) + near + from_far.astype(jnp.float32)


def dp_bits(count):
    low = [1 << k for k in range(count.bit_length() - 1)]
    if count == 64:
        return [low[0], low[4]], [low[1], low[2], low[3], low[5]]
    return [], low


def attend(queries, attn_keys, values):
    prompt_count = queries.shape[0]
    seq_length = queries.shape[1]
    local_kv = attn_keys.shape[2] // HDIM
    local_heads = queries.shape[2] // HDIM
    group_size = local_heads // local_kv
    query_blocks = queries.reshape(prompt_count, seq_length, local_kv, group_size, HDIM)
    key_blocks = attn_keys.reshape(prompt_count, seq_length, local_kv, HDIM)
    value_blocks = values.reshape(prompt_count, seq_length, local_kv, HDIM)
    scores = jnp.einsum(
        "pqkgd,pskd->pkgqs", query_blocks, key_blocks, preferred_element_type=jnp.float32
    ) / math.sqrt(HDIM)
    causal = jnp.arange(seq_length)[:, None] >= jnp.arange(seq_length)[None, :]
    scores = jnp.where(causal, scores, -jnp.inf)
    highest = jnp.max(scores, axis=-1, keepdims=True)
    exponent = jnp.exp(scores - highest)
    weights = (exponent / jnp.sum(exponent, axis=-1, keepdims=True)).astype(jnp.bfloat16)
    mixed_rows = jnp.einsum(
        "pkgqs,pskd->pqkgd", weights, value_blocks, preferred_element_type=jnp.float32
    )
    return mixed_rows.astype(jnp.bfloat16).reshape(prompt_count, seq_length, local_heads, HDIM)


def attend_rows(queries, attn_keys, values, pick_values, head_ids, pos_ids):
    prompt_count = queries.shape[0]
    seq_length = queries.shape[1]
    local_kv = attn_keys.shape[2] // HDIM
    local_heads = queries.shape[2] // HDIM
    group_size = local_heads // local_kv
    query_rows = jnp.einsum(
        "jkr,jrd->jkd",
        pick_values,
        queries.reshape(prompt_count, seq_length * local_heads, HDIM),
        preferred_element_type=jnp.float32,
    ).astype(queries.dtype)
    key_blocks = attn_keys.reshape(prompt_count, seq_length, local_kv, HDIM)
    value_blocks = values.reshape(prompt_count, seq_length, local_kv, HDIM)
    kv_pick = (
        (head_ids // group_size)[:, :, None] == jnp.arange(local_kv, dtype=head_ids.dtype)[None, None, :]
    ).astype(jnp.float32)
    all_scores = jnp.einsum(
        "jkd,jsvd->jksv", query_rows, key_blocks, preferred_element_type=jnp.float32
    )
    scores = jnp.sum(all_scores * kv_pick[:, :, None, :], axis=-1) / math.sqrt(HDIM)
    causal = jnp.arange(seq_length)[None, None, :] <= pos_ids[:, :, None]
    scores = jnp.where(causal, scores, -jnp.inf)
    highest = jnp.max(scores, axis=-1, keepdims=True)
    exponent = jnp.exp(scores - highest)
    weights = (exponent / jnp.sum(exponent, axis=-1, keepdims=True)).astype(jnp.bfloat16)
    all_rows = jnp.einsum(
        "jks,jsvd->jkvd", weights, value_blocks, preferred_element_type=jnp.float32
    )
    mixed = jnp.sum(all_rows * kv_pick[..., None], axis=2)
    return mixed.astype(jnp.bfloat16)


def per_device(
    residual,
    queries,
    attn_keys,
    values,
    out_weight,
    norm_gain,
    probe_weight,
    partner_slot,
    patch_list,
    concept_labels,
):
    prompt_count = residual.shape[0]
    seq_length = residual.shape[1]
    feature_count = residual.shape[2]
    token_count = prompt_count * seq_length
    local_heads = queries.shape[2] // HDIM
    rows = seq_length * local_heads

    entry_rows = patch_list[..., 1] * local_heads + patch_list[..., 0] % local_heads
    picks = entry_rows[:, :, None] == jnp.arange(rows, dtype=jnp.int32)[None, None, :]
    pick_values = picks.astype(jnp.bfloat16)
    own_entries = attend_rows(
        queries, attn_keys, values, pick_values, patch_list[..., 0] % local_heads, patch_list[..., 1]
    )
    heads_out = attend(queries, attn_keys, values)
    flat_heads = heads_out.reshape(prompt_count, rows, HDIM)

    half_way = lax.axis_size("dp") // 2
    arrived = exchanged(own_entries, "dp", half_way)
    slot_pick = (
        partner_slot[:, None] == jnp.arange(prompt_count, dtype=partner_slot.dtype)[None, :]
    ).astype(jnp.bfloat16)
    incoming = jnp.einsum(
        "jm,mkd->jkd", slot_pick, arrived, preferred_element_type=jnp.float32
    ).astype(jnp.bfloat16)
    patch_mask = jnp.any(picks, axis=1)
    flat_residual = residual.reshape(token_count, feature_count)
    chunk_count = 2 if prompt_count % 2 == 0 else 1
    chunk = token_count // chunk_count
    prompts_per_chunk = prompt_count // chunk_count
    patched_chunks = []
    for index in range(chunk_count):
        prompts_here = slice(index * prompts_per_chunk, (index + 1) * prompts_per_chunk)
        placed = jnp.einsum(
            "jkr,jkd->jrd",
            pick_values[prompts_here],
            incoming[prompts_here],
            preferred_element_type=jnp.float32,
        ).astype(jnp.bfloat16)
        patched_here = jnp.where(
            patch_mask[prompts_here][..., None], placed, flat_heads[prompts_here]
        )
        patched_chunks.append(patched_here.reshape(chunk, -1))
    labels = concept_labels.reshape(token_count)
    concepts = probe_weight.shape[1]
    tensor_bits = [1 << k for k in range(lax.axis_size("tensor").bit_length() - 1)]
    halves, sent_block = [], None
    for index in range(chunk_count):
        rows_here = slice(index * chunk, (index + 1) * chunk)
        heads_here, sent_block, from_far = far_half(
            patched_chunks[index], out_weight, "tensor", sent_block
        )
        halves.append((heads_here, sent_block, from_far))
    attn_chunks, logit_chunks, grad_local = [], [], None
    for index in range(chunk_count):
        rows_here = slice(index * chunk, (index + 1) * chunk)
        heads_here, _, from_far = halves[index]
        if index + 1 < chunk_count:
            from_far, _ = lax.optimization_barrier((from_far, halves[index + 1][1]))
        attn_local = near_half(heads_here, out_weight, "tensor", from_far).astype(jnp.bfloat16)
        hidden = flat_residual[rows_here].astype(jnp.float32) + attn_local.astype(jnp.float32)
        square_local = jnp.sum(hidden * hidden, axis=1)
        scaled = hidden * norm_gain
        raw_part = jnp.dot(
            scaled, probe_weight, precision=lax.Precision.HIGH, preferred_element_type=jnp.float32
        )
        packed = jnp.concatenate([raw_part, square_local[:, None]], axis=1)
        packed = butterfly_sum(packed, "tensor", tensor_bits)
        inverse_rms = lax.rsqrt(packed[:, concepts] / DW + norm_epsilon)
        logits = packed[:, :concepts] * inverse_rms[:, None]
        normed = scaled * inverse_rms[:, None]
        classes = jnp.arange(concepts, dtype=jnp.int32)
        target = (labels[rows_here][:, None] == classes[None, :]).astype(jnp.float32)
        error = jax.nn.sigmoid(logits) - target
        grad_part = lax.dot_general(
            normed,
            error,
            (((0,), (0,)), ((), ())),
            precision=lax.Precision.HIGH,
            preferred_element_type=jnp.float32,
        )
        grad_local = grad_part if grad_local is None else grad_local + grad_part
        attn_chunks.append(attn_local)
        logit_chunks.append(logits)
    attn_local = jnp.concatenate(attn_chunks, axis=0)
    logits = jnp.concatenate(logit_chunks, axis=0)
    total_tokens = token_count * lax.axis_size("dp")
    grad_local = grad_local / math.sqrt(total_tokens)
    halving_bits, doubling_bits = dp_bits(lax.axis_size("dp"))
    probe_grad = tree_all_reduce(grad_local, "dp", halving_bits, doubling_bits)
    return (
        attn_local.reshape(prompt_count, seq_length, feature_count),
        logits.reshape(prompt_count, seq_length, -1),
        probe_grad,
    )


def solution(mesh):
    return jax.shard_map(
        per_device,
        mesh=mesh,
        in_specs=(
            P("dp", None, "tensor"),
            P("dp", None, "tensor"),
            P("dp", None, "tensor"),
            P("dp", None, "tensor"),
            P("tensor", None),
            P("tensor"),
            P("tensor", None),
            P("dp"),
            P("dp", "tensor", None),
            P("dp", None),
        ),
        out_specs=(P("dp", None, "tensor"), P("dp", None, None), P("tensor", None)),
        check_vma=False,
    )
```

```python
import math

import jax
import jax.numpy as jnp
from jax import lax
from jax.sharding import PartitionSpec as P

DW = 4096
HDIM = 128


norm_epsilon = 1e-05


def exchanged(block, axis, bit):
    count = lax.axis_size(axis)
    return lax.ppermute(block, axis, [(i, i ^ bit) for i in range(count)])


def butterfly_sum(block, axis, bits):
    for bit in bits:
        block = block + exchanged(block, axis, bit)
    return block


def tree_all_reduce(block, axis, halving_bits, doubling_bits):
    position = lax.axis_index(axis)
    kept = []
    for bit in halving_bits:
        half = block.shape[0] // 2
        upper = (position // bit) % 2 == 1
        low, high = block[:half], block[half:]
        mine = jnp.where(upper, high, low)
        other = jnp.where(upper, low, high)
        block = mine + exchanged(other, axis, bit)
        kept.append((bit, upper))
    block = butterfly_sum(block, axis, doubling_bits)
    for bit, upper in reversed(kept):
        other = exchanged(block, axis, bit)
        block = jnp.where(upper, jnp.concatenate([other, block]), jnp.concatenate([block, other]))
    return block


def far_half(heads, weight, axis, after=None):
    count = lax.axis_size(axis)
    position = lax.axis_index(axis)
    width = weight.shape[1] // count
    if after is not None:
        heads, _ = lax.optimization_barrier((heads, after))

    def block(index):
        columns = lax.dynamic_slice_in_dim(weight, index * width, width, axis=1)
        return jnp.dot(heads, columns, preferred_element_type=jnp.float32)

    def sent(value, bit):
        return exchanged(value.astype(jnp.bfloat16), axis, bit).astype(jnp.float32)

    far = position ^ 2
    partner_share = block(far ^ 1).astype(jnp.bfloat16)
    from_partner = exchanged(partner_share, axis, 1).astype(jnp.float32)
    far_sum = (block(far) + from_partner).astype(jnp.bfloat16)
    heads, far_sum = lax.optimization_barrier((heads, far_sum))
    return heads, partner_share, exchanged(far_sum, axis, 2)


def near_half(heads, weight, axis, from_far):
    count = lax.axis_size(axis)
    position = lax.axis_index(axis)
    width = weight.shape[1] // count

    def block(index):
        columns = lax.dynamic_slice_in_dim(weight, index * width, width, axis=1)
        return jnp.dot(heads, columns, preferred_element_type=jnp.float32)

    near = exchanged(block(position ^ 1).astype(jnp.bfloat16), axis, 1).astype(jnp.float32)
    return block(position) + near + from_far.astype(jnp.float32)


def dp_bits(count):
    low = [1 << k for k in range(count.bit_length() - 1)]
    if count == 64:
        return [low[0], low[4]], [low[1], low[1] | low[2], low[3], low[5]]
    return [], low


def attend(queries, attn_keys, values):
    prompt_count = queries.shape[0]
    seq_length = queries.shape[1]
    local_kv = attn_keys.shape[2] // HDIM
    local_heads = queries.shape[2] // HDIM
    group_size = local_heads // local_kv
    query_blocks = queries.reshape(prompt_count, seq_length, local_kv, group_size, HDIM)
    key_blocks = attn_keys.reshape(prompt_count, seq_length, local_kv, HDIM)
    value_blocks = values.reshape(prompt_count, seq_length, local_kv, HDIM)
    scores = jnp.einsum(
        "pqkgd,pskd->pkgqs", query_blocks, key_blocks, preferred_element_type=jnp.float32
    ) / math.sqrt(HDIM)
    causal = jnp.arange(seq_length)[:, None] >= jnp.arange(seq_length)[None, :]
    scores = jnp.where(causal, scores, -jnp.inf)
    highest = jnp.max(scores, axis=-1, keepdims=True)
    exponent = jnp.exp(scores - highest)
    weights = (exponent / jnp.sum(exponent, axis=-1, keepdims=True)).astype(jnp.bfloat16)
    mixed_rows = jnp.einsum(
        "pkgqs,pskd->pqkgd", weights, value_blocks, preferred_element_type=jnp.float32
    )
    return mixed_rows.astype(jnp.bfloat16).reshape(prompt_count, seq_length, local_heads, HDIM)


def attend_rows(queries, attn_keys, values, pick_values, head_ids, pos_ids):
    prompt_count = queries.shape[0]
    seq_length = queries.shape[1]
    local_kv = attn_keys.shape[2] // HDIM
    local_heads = queries.shape[2] // HDIM
    group_size = local_heads // local_kv
    query_rows = jnp.einsum(
        "jkr,jrd->jkd",
        pick_values,
        queries.reshape(prompt_count, seq_length * local_heads, HDIM),
        preferred_element_type=jnp.float32,
    ).astype(queries.dtype)
    key_blocks = attn_keys.reshape(prompt_count, seq_length, local_kv, HDIM)
    value_blocks = values.reshape(prompt_count, seq_length, local_kv, HDIM)
    kv_pick = (
        (head_ids // group_size)[:, :, None] == jnp.arange(local_kv, dtype=head_ids.dtype)[None, None, :]
    ).astype(jnp.float32)
    all_scores = jnp.einsum(
        "jkd,jsvd->jksv", query_rows, key_blocks, preferred_element_type=jnp.float32
    )
    scores = jnp.sum(all_scores * kv_pick[:, :, None, :], axis=-1) / math.sqrt(HDIM)
    causal = jnp.arange(seq_length)[None, None, :] <= pos_ids[:, :, None]
    scores = jnp.where(causal, scores, -jnp.inf)
    highest = jnp.max(scores, axis=-1, keepdims=True)
    exponent = jnp.exp(scores - highest)
    weights = (exponent / jnp.sum(exponent, axis=-1, keepdims=True)).astype(jnp.bfloat16)
    all_rows = jnp.einsum(
        "jks,jsvd->jkvd", weights, value_blocks, preferred_element_type=jnp.float32
    )
    mixed = jnp.sum(all_rows * kv_pick[..., None], axis=2)
    return mixed.astype(jnp.bfloat16)


def per_device(
    residual,
    queries,
    attn_keys,
    values,
    out_weight,
    norm_gain,
    probe_weight,
    partner_slot,
    patch_list,
    concept_labels,
):
    prompt_count = residual.shape[0]
    seq_length = residual.shape[1]
    feature_count = residual.shape[2]
    token_count = prompt_count * seq_length
    local_heads = queries.shape[2] // HDIM
    rows = seq_length * local_heads

    entry_rows = patch_list[..., 1] * local_heads + patch_list[..., 0] % local_heads
    picks = entry_rows[:, :, None] == jnp.arange(rows, dtype=jnp.int32)[None, None, :]
    pick_values = picks.astype(jnp.bfloat16)
    own_entries = attend_rows(
        queries, attn_keys, values, pick_values, patch_list[..., 0] % local_heads, patch_list[..., 1]
    )
    heads_out = attend(queries, attn_keys, values)
    flat_heads = heads_out.reshape(prompt_count, rows, HDIM)

    half_way = lax.axis_size("dp") // 2
    arrived = exchanged(own_entries, "dp", half_way)
    slot_pick = (
        partner_slot[:, None] == jnp.arange(prompt_count, dtype=partner_slot.dtype)[None, :]
    ).astype(jnp.bfloat16)
    incoming = jnp.einsum(
        "jm,mkd->jkd", slot_pick, arrived, preferred_element_type=jnp.float32
    ).astype(jnp.bfloat16)
    patch_mask = jnp.any(picks, axis=1)
    flat_residual = residual.reshape(token_count, feature_count)
    chunk_count = 2 if prompt_count % 2 == 0 else 1
    chunk = token_count // chunk_count
    prompts_per_chunk = prompt_count // chunk_count
    patched_chunks = []
    for index in range(chunk_count):
        prompts_here = slice(index * prompts_per_chunk, (index + 1) * prompts_per_chunk)
        placed = jnp.einsum(
            "jkr,jkd->jrd",
            pick_values[prompts_here],
            incoming[prompts_here],
            preferred_element_type=jnp.float32,
        ).astype(jnp.bfloat16)
        patched_here = jnp.where(
            patch_mask[prompts_here][..., None], placed, flat_heads[prompts_here]
        )
        patched_chunks.append(patched_here.reshape(chunk, -1))
    labels = concept_labels.reshape(token_count)
    concepts = probe_weight.shape[1]
    tensor_bits = [1 << k for k in range(lax.axis_size("tensor").bit_length() - 1)]
    halves, sent_block = [], None
    for index in range(chunk_count):
        rows_here = slice(index * chunk, (index + 1) * chunk)
        heads_here, sent_block, from_far = far_half(
            patched_chunks[index], out_weight, "tensor", sent_block
        )
        halves.append((heads_here, sent_block, from_far))
    attn_chunks, logit_chunks, grad_local = [], [], None
    for index in range(chunk_count):
        rows_here = slice(index * chunk, (index + 1) * chunk)
        heads_here, _, from_far = halves[index]
        if index + 1 < chunk_count:
            from_far, _ = lax.optimization_barrier((from_far, halves[index + 1][1]))
        attn_local = near_half(heads_here, out_weight, "tensor", from_far).astype(jnp.bfloat16)
        hidden = flat_residual[rows_here].astype(jnp.float32) + attn_local.astype(jnp.float32)
        square_local = jnp.sum(hidden * hidden, axis=1)
        scaled = hidden * norm_gain
        raw_part = jnp.dot(
            scaled, probe_weight, precision=lax.Precision.HIGH, preferred_element_type=jnp.float32
        )
        packed = jnp.concatenate([raw_part, square_local[:, None]], axis=1)
        packed = butterfly_sum(packed, "tensor", tensor_bits)
        inverse_rms = lax.rsqrt(packed[:, concepts] / DW + norm_epsilon)
        logits = packed[:, :concepts] * inverse_rms[:, None]
        normed = scaled * inverse_rms[:, None]
        classes = jnp.arange(concepts, dtype=jnp.int32)
        target = (labels[rows_here][:, None] == classes[None, :]).astype(jnp.float32)
        error = jax.nn.sigmoid(logits) - target
        grad_part = lax.dot_general(
            normed,
            error,
            (((0,), (0,)), ((), ())),
            precision=lax.Precision.HIGH,
            preferred_element_type=jnp.float32,
        )
        grad_local = grad_part if grad_local is None else grad_local + grad_part
        attn_chunks.append(attn_local)
        logit_chunks.append(logits)
    attn_local = jnp.concatenate(attn_chunks, axis=0)
    logits = jnp.concatenate(logit_chunks, axis=0)
    total_tokens = token_count * lax.axis_size("dp")
    grad_local = grad_local / math.sqrt(total_tokens)
    halving_bits, doubling_bits = dp_bits(lax.axis_size("dp"))
    probe_grad = tree_all_reduce(grad_local, "dp", halving_bits, doubling_bits)
    return (
        attn_local.reshape(prompt_count, seq_length, feature_count),
        logits.reshape(prompt_count, seq_length, -1),
        probe_grad,
    )


def solution(mesh):
    return jax.shard_map(
        per_device,
        mesh=mesh,
        in_specs=(
            P("dp", None, "tensor"),
            P("dp", None, "tensor"),
            P("dp", None, "tensor"),
            P("dp", None, "tensor"),
            P("tensor", None),
            P("tensor"),
            P("tensor", None),
            P("dp"),
            P("dp", "tensor", None),
            P("dp", None),
        ),
        out_specs=(P("dp", None, "tensor"), P("dp", None, None), P("tensor", None)),
        check_vma=False,
    )
```

```python
import math

import jax
import jax.numpy as jnp
from jax import lax
from jax.sharding import PartitionSpec as P

DW = 4096
HDIM = 128


norm_epsilon = 1e-05


def exchanged(block, axis, bit):
    count = lax.axis_size(axis)
    return lax.ppermute(block, axis, [(i, i ^ bit) for i in range(count)])


def butterfly_sum(block, axis, bits):
    for bit in bits:
        block = block + exchanged(block, axis, bit)
    return block


def tree_all_reduce(block, axis, halving_bits, doubling_bits):
    position = lax.axis_index(axis)
    kept = []
    for bit in halving_bits:
        half = block.shape[0] // 2
        upper = (position // bit) % 2 == 1
        low, high = block[:half], block[half:]
        mine = jnp.where(upper, high, low)
        other = jnp.where(upper, low, high)
        block = mine + exchanged(other, axis, bit)
        kept.append((bit, upper))
    block = butterfly_sum(block, axis, doubling_bits)
    for bit, upper in reversed(kept):
        other = exchanged(block, axis, bit)
        block = jnp.where(upper, jnp.concatenate([other, block]), jnp.concatenate([block, other]))
    return block


def far_half(heads, weight, axis, after=None):
    count = lax.axis_size(axis)
    position = lax.axis_index(axis)
    width = weight.shape[1] // count
    if after is not None:
        heads, _ = lax.optimization_barrier((heads, after))

    def block(index):
        columns = lax.dynamic_slice_in_dim(weight, index * width, width, axis=1)
        return jnp.dot(heads, columns, preferred_element_type=jnp.float32)

    def sent(value, bit):
        return exchanged(value.astype(jnp.bfloat16), axis, bit).astype(jnp.float32)

    far = position ^ 2
    partner_share = block(far ^ 1).astype(jnp.bfloat16)
    from_partner = exchanged(partner_share, axis, 1).astype(jnp.float32)
    far_sum = (block(far) + from_partner).astype(jnp.bfloat16)
    heads, far_sum = lax.optimization_barrier((heads, far_sum))
    return heads, partner_share, exchanged(far_sum, axis, 2)


def near_half(heads, weight, axis, from_far):
    count = lax.axis_size(axis)
    position = lax.axis_index(axis)
    width = weight.shape[1] // count

    def block(index):
        columns = lax.dynamic_slice_in_dim(weight, index * width, width, axis=1)
        return jnp.dot(heads, columns, preferred_element_type=jnp.float32)

    near = exchanged(block(position ^ 1).astype(jnp.bfloat16), axis, 1).astype(jnp.float32)
    return block(position) + near + from_far.astype(jnp.float32)


def dp_bits(count):
    low = [1 << k for k in range(count.bit_length() - 1)]
    if count == 64:
        return [low[0], low[4]], [low[1], low[1] | low[2], low[3], low[5]]
    return [], low


def attend(queries, attn_keys, values):
    prompt_count = queries.shape[0]
    seq_length = queries.shape[1]
    local_kv = attn_keys.shape[2] // HDIM
    local_heads = queries.shape[2] // HDIM
    group_size = local_heads // local_kv
    query_blocks = queries.reshape(prompt_count, seq_length, local_kv, group_size, HDIM)
    key_blocks = attn_keys.reshape(prompt_count, seq_length, local_kv, HDIM)
    value_blocks = values.reshape(prompt_count, seq_length, local_kv, HDIM)
    scores = jnp.einsum(
        "pqkgd,pskd->pkgqs", query_blocks, key_blocks, preferred_element_type=jnp.float32
    ) / math.sqrt(HDIM)
    causal = jnp.arange(seq_length)[:, None] >= jnp.arange(seq_length)[None, :]
    scores = jnp.where(causal, scores, -jnp.inf)
    highest = jnp.max(scores, axis=-1, keepdims=True)
    exponent = jnp.exp(scores - highest)
    weights = (exponent / jnp.sum(exponent, axis=-1, keepdims=True)).astype(jnp.bfloat16)
    mixed_rows = jnp.einsum(
        "pkgqs,pskd->pqkgd", weights, value_blocks, preferred_element_type=jnp.float32
    )
    return mixed_rows.astype(jnp.bfloat16).reshape(prompt_count, seq_length, local_heads, HDIM)


def attend_rows(queries, attn_keys, values, pick_values, head_ids, pos_ids):
    prompt_count = queries.shape[0]
    seq_length = queries.shape[1]
    local_kv = attn_keys.shape[2] // HDIM
    local_heads = queries.shape[2] // HDIM
    group_size = local_heads // local_kv
    pos_pick = (
        pos_ids[:, :, None] == jnp.arange(seq_length, dtype=pos_ids.dtype)[None, None, :]
    ).astype(queries.dtype)
    head_pick = (
        head_ids[:, :, None] == jnp.arange(local_heads, dtype=head_ids.dtype)[None, None, :]
    ).astype(queries.dtype)
    query_lines = jnp.einsum(
        "jks,jsf->jkf", pos_pick, queries, preferred_element_type=jnp.float32
    ).astype(queries.dtype)
    query_rows = jnp.einsum(
        "jkh,jkhd->jkd",
        head_pick,
        query_lines.reshape(prompt_count, -1, local_heads, HDIM),
        preferred_element_type=jnp.float32,
    ).astype(queries.dtype)
    key_blocks = attn_keys.reshape(prompt_count, seq_length, local_kv, HDIM)
    value_blocks = values.reshape(prompt_count, seq_length, local_kv, HDIM)
    kv_pick = (
        (head_ids // group_size)[:, :, None] == jnp.arange(local_kv, dtype=head_ids.dtype)[None, None, :]
    ).astype(jnp.float32)
    all_scores = jnp.einsum(
        "jkd,jsvd->jksv", query_rows, key_blocks, preferred_element_type=jnp.float32
    )
    scores = jnp.sum(all_scores * kv_pick[:, :, None, :], axis=-1) / math.sqrt(HDIM)
    causal = jnp.arange(seq_length)[None, None, :] <= pos_ids[:, :, None]
    scores = jnp.where(causal, scores, -jnp.inf)
    highest = jnp.max(scores, axis=-1, keepdims=True)
    exponent = jnp.exp(scores - highest)
    weights = (exponent / jnp.sum(exponent, axis=-1, keepdims=True)).astype(jnp.bfloat16)
    all_rows = jnp.einsum(
        "jks,jsvd->jkvd", weights, value_blocks, preferred_element_type=jnp.float32
    )
    mixed = jnp.sum(all_rows * kv_pick[..., None], axis=2)
    return mixed.astype(jnp.bfloat16)


def per_device(
    residual,
    queries,
    attn_keys,
    values,
    out_weight,
    norm_gain,
    probe_weight,
    partner_slot,
    patch_list,
    concept_labels,
):
    prompt_count = residual.shape[0]
    seq_length = residual.shape[1]
    feature_count = residual.shape[2]
    token_count = prompt_count * seq_length
    local_heads = queries.shape[2] // HDIM
    rows = seq_length * local_heads

    entry_rows = patch_list[..., 1] * local_heads + patch_list[..., 0] % local_heads
    picks = entry_rows[:, :, None] == jnp.arange(rows, dtype=jnp.int32)[None, None, :]
    pick_values = picks.astype(jnp.bfloat16)
    own_entries = attend_rows(
        queries, attn_keys, values, pick_values, patch_list[..., 0] % local_heads, patch_list[..., 1]
    )
    heads_out = attend(queries, attn_keys, values)
    flat_heads = heads_out.reshape(prompt_count, rows, HDIM)

    half_way = lax.axis_size("dp") // 2
    arrived = exchanged(own_entries, "dp", half_way)
    slot_pick = (
        partner_slot[:, None] == jnp.arange(prompt_count, dtype=partner_slot.dtype)[None, :]
    ).astype(jnp.bfloat16)
    incoming = jnp.einsum(
        "jm,mkd->jkd", slot_pick, arrived, preferred_element_type=jnp.float32
    ).astype(jnp.bfloat16)
    patch_mask = jnp.any(picks, axis=1)
    flat_residual = residual.reshape(token_count, feature_count)
    chunk_count = 2 if prompt_count % 2 == 0 else 1
    chunk = token_count // chunk_count
    prompts_per_chunk = prompt_count // chunk_count
    patched_chunks = []
    for index in range(chunk_count):
        prompts_here = slice(index * prompts_per_chunk, (index + 1) * prompts_per_chunk)
        placed = jnp.einsum(
            "jkr,jkd->jrd",
            pick_values[prompts_here],
            incoming[prompts_here],
            preferred_element_type=jnp.float32,
        ).astype(jnp.bfloat16)
        patched_here = jnp.where(
            patch_mask[prompts_here][..., None], placed, flat_heads[prompts_here]
        )
        patched_chunks.append(patched_here.reshape(chunk, -1))
    labels = concept_labels.reshape(token_count)
    concepts = probe_weight.shape[1]
    tensor_bits = [1 << k for k in range(lax.axis_size("tensor").bit_length() - 1)]
    halves, sent_block = [], None
    for index in range(chunk_count):
        rows_here = slice(index * chunk, (index + 1) * chunk)
        heads_here, sent_block, from_far = far_half(
            patched_chunks[index], out_weight, "tensor", sent_block
        )
        halves.append((heads_here, sent_block, from_far))
    attn_chunks, logit_chunks, grad_local = [], [], None
    for index in range(chunk_count):
        rows_here = slice(index * chunk, (index + 1) * chunk)
        heads_here, _, from_far = halves[index]
        if index + 1 < chunk_count:
            from_far, _ = lax.optimization_barrier((from_far, halves[index + 1][1]))
        attn_local = near_half(heads_here, out_weight, "tensor", from_far).astype(jnp.bfloat16)
        hidden = flat_residual[rows_here].astype(jnp.float32) + attn_local.astype(jnp.float32)
        square_local = jnp.sum(hidden * hidden, axis=1)
        scaled = hidden * norm_gain
        raw_part = jnp.dot(
            scaled, probe_weight, precision=lax.Precision.HIGH, preferred_element_type=jnp.float32
        )
        packed = jnp.concatenate([raw_part, square_local[:, None]], axis=1)
        packed = butterfly_sum(packed, "tensor", tensor_bits)
        inverse_rms = lax.rsqrt(packed[:, concepts] / DW + norm_epsilon)
        logits = packed[:, :concepts] * inverse_rms[:, None]
        normed = scaled * inverse_rms[:, None]
        classes = jnp.arange(concepts, dtype=jnp.int32)
        target = (labels[rows_here][:, None] == classes[None, :]).astype(jnp.float32)
        error = jax.nn.sigmoid(logits) - target
        grad_part = lax.dot_general(
            normed,
            error,
            (((0,), (0,)), ((), ())),
            precision=lax.Precision.HIGH,
            preferred_element_type=jnp.float32,
        )
        grad_local = grad_part if grad_local is None else grad_local + grad_part
        attn_chunks.append(attn_local)
        logit_chunks.append(logits)
    attn_local = jnp.concatenate(attn_chunks, axis=0)
    logits = jnp.concatenate(logit_chunks, axis=0)
    total_tokens = token_count * lax.axis_size("dp")
    grad_local = grad_local / math.sqrt(total_tokens)
    halving_bits, doubling_bits = dp_bits(lax.axis_size("dp"))
    probe_grad = tree_all_reduce(grad_local, "dp", halving_bits, doubling_bits)
    return (
        attn_local.reshape(prompt_count, seq_length, feature_count),
        logits.reshape(prompt_count, seq_length, -1),
        probe_grad,
    )


def solution(mesh):
    return jax.shard_map(
        per_device,
        mesh=mesh,
        in_specs=(
            P("dp", None, "tensor"),
            P("dp", None, "tensor"),
            P("dp", None, "tensor"),
            P("dp", None, "tensor"),
            P("tensor", None),
            P("tensor"),
            P("tensor", None),
            P("dp"),
            P("dp", "tensor", None),
            P("dp", None),
        ),
        out_specs=(P("dp", None, "tensor"), P("dp", None, None), P("tensor", None)),
        check_vma=False,
    )
```

```python
import math

import jax
import jax.numpy as jnp
from jax import lax
from jax.sharding import PartitionSpec as P

DW = 4096
HDIM = 128


norm_epsilon = 1e-05


def exchanged(block, axis, bit):
    count = lax.axis_size(axis)
    return lax.ppermute(block, axis, [(i, i ^ bit) for i in range(count)])


def butterfly_sum(block, axis, bits):
    for bit in bits:
        block = block + exchanged(block, axis, bit)
    return block


def tree_all_reduce(block, axis, halving_bits, doubling_bits):
    position = lax.axis_index(axis)
    kept = []
    for bit in halving_bits:
        half = block.shape[0] // 2
        upper = (position // bit) % 2 == 1
        low, high = block[:half], block[half:]
        mine = jnp.where(upper, high, low)
        other = jnp.where(upper, low, high)
        block = mine + exchanged(other, axis, bit)
        kept.append((bit, upper))
    block = butterfly_sum(block, axis, doubling_bits)
    for bit, upper in reversed(kept):
        other = exchanged(block, axis, bit)
        block = jnp.concatenate([jnp.where(upper, other, block), jnp.where(upper, block, other)])
    return block


def far_half(heads, weight, axis, after=None):
    count = lax.axis_size(axis)
    position = lax.axis_index(axis)
    width = weight.shape[1] // count
    if after is not None:
        heads, _ = lax.optimization_barrier((heads, after))

    def block(index):
        columns = lax.dynamic_slice_in_dim(weight, index * width, width, axis=1)
        return jnp.dot(heads, columns, preferred_element_type=jnp.float32)

    def sent(value, bit):
        return exchanged(value.astype(jnp.bfloat16), axis, bit).astype(jnp.float32)

    far = position ^ 2
    partner_share = block(far ^ 1).astype(jnp.bfloat16)
    from_partner = exchanged(partner_share, axis, 1).astype(jnp.float32)
    far_sum = (block(far) + from_partner).astype(jnp.bfloat16)
    heads, far_sum = lax.optimization_barrier((heads, far_sum))
    return heads, partner_share, exchanged(far_sum, axis, 2)


def near_half(heads, weight, axis, from_far):
    count = lax.axis_size(axis)
    position = lax.axis_index(axis)
    width = weight.shape[1] // count

    def block(index):
        columns = lax.dynamic_slice_in_dim(weight, index * width, width, axis=1)
        return jnp.dot(heads, columns, preferred_element_type=jnp.float32)

    near = exchanged(block(position ^ 1).astype(jnp.bfloat16), axis, 1).astype(jnp.float32)
    return block(position) + near + from_far.astype(jnp.float32)


def dp_bits(count):
    low = [1 << k for k in range(count.bit_length() - 1)]
    if count == 64:
        return [low[0], low[4]], [low[1], low[1] | low[2], low[3], low[5]]
    return [], low


def attend(queries, attn_keys, values):
    prompt_count = queries.shape[0]
    seq_length = queries.shape[1]
    local_kv = attn_keys.shape[2] // HDIM
    local_heads = queries.shape[2] // HDIM
    group_size = local_heads // local_kv
    query_blocks = queries.reshape(prompt_count, seq_length, local_kv, group_size, HDIM)
    key_blocks = attn_keys.reshape(prompt_count, seq_length, local_kv, HDIM)
    value_blocks = values.reshape(prompt_count, seq_length, local_kv, HDIM)
    scores = jnp.einsum(
        "pqkgd,pskd->pkgqs", query_blocks, key_blocks, preferred_element_type=jnp.float32
    ) / math.sqrt(HDIM)
    causal = jnp.arange(seq_length)[:, None] >= jnp.arange(seq_length)[None, :]
    scores = jnp.where(causal, scores, -jnp.inf)
    highest = jnp.max(scores, axis=-1, keepdims=True)
    exponent = jnp.exp(scores - highest)
    weights = (exponent / jnp.sum(exponent, axis=-1, keepdims=True)).astype(jnp.bfloat16)
    mixed_rows = jnp.einsum(
        "pkgqs,pskd->pqkgd", weights, value_blocks, preferred_element_type=jnp.float32
    )
    return mixed_rows.astype(jnp.bfloat16).reshape(prompt_count, seq_length, local_heads, HDIM)


def attend_rows(queries, attn_keys, values, pick_values, head_ids, pos_ids):
    prompt_count = queries.shape[0]
    seq_length = queries.shape[1]
    local_kv = attn_keys.shape[2] // HDIM
    local_heads = queries.shape[2] // HDIM
    group_size = local_heads // local_kv
    query_rows = jnp.einsum(
        "jkr,jrd->jkd",
        pick_values,
        queries.reshape(prompt_count, seq_length * local_heads, HDIM),
        preferred_element_type=jnp.float32,
    ).astype(queries.dtype)
    key_blocks = attn_keys.reshape(prompt_count, seq_length, local_kv, HDIM)
    value_blocks = values.reshape(prompt_count, seq_length, local_kv, HDIM)
    kv_pick = (
        (head_ids // group_size)[:, :, None] == jnp.arange(local_kv, dtype=head_ids.dtype)[None, None, :]
    ).astype(jnp.float32)
    all_scores = jnp.einsum(
        "jkd,jsvd->jksv", query_rows, key_blocks, preferred_element_type=jnp.float32
    )
    scores = jnp.sum(all_scores * kv_pick[:, :, None, :], axis=-1) / math.sqrt(HDIM)
    causal = jnp.arange(seq_length)[None, None, :] <= pos_ids[:, :, None]
    scores = jnp.where(causal, scores, -jnp.inf)
    highest = jnp.max(scores, axis=-1, keepdims=True)
    exponent = jnp.exp(scores - highest)
    weights = (exponent / jnp.sum(exponent, axis=-1, keepdims=True)).astype(jnp.bfloat16)
    all_rows = jnp.einsum(
        "jks,jsvd->jkvd", weights, value_blocks, preferred_element_type=jnp.float32
    )
    mixed = jnp.sum(all_rows * kv_pick[..., None], axis=2)
    return mixed.astype(jnp.bfloat16)


def per_device(
    residual,
    queries,
    attn_keys,
    values,
    out_weight,
    norm_gain,
    probe_weight,
    partner_slot,
    patch_list,
    concept_labels,
):
    prompt_count = residual.shape[0]
    seq_length = residual.shape[1]
    feature_count = residual.shape[2]
    token_count = prompt_count * seq_length
    local_heads = queries.shape[2] // HDIM
    rows = seq_length * local_heads

    entry_rows = patch_list[..., 1] * local_heads + patch_list[..., 0] % local_heads
    picks = entry_rows[:, :, None] == jnp.arange(rows, dtype=jnp.int32)[None, None, :]
    pick_values = picks.astype(jnp.bfloat16)
    own_entries = attend_rows(
        queries, attn_keys, values, pick_values, patch_list[..., 0] % local_heads, patch_list[..., 1]
    )
    heads_out = attend(queries, attn_keys, values)
    flat_heads = heads_out.reshape(prompt_count, rows, HDIM)

    half_way = lax.axis_size("dp") // 2
    arrived = exchanged(own_entries, "dp", half_way)
    slot_pick = (
        partner_slot[:, None] == jnp.arange(prompt_count, dtype=partner_slot.dtype)[None, :]
    ).astype(jnp.bfloat16)
    incoming = jnp.einsum(
        "jm,mkd->jkd", slot_pick, arrived, preferred_element_type=jnp.float32
    ).astype(jnp.bfloat16)
    patch_mask = jnp.any(picks, axis=1)
    flat_residual = residual.reshape(token_count, feature_count)
    chunk_count = 2 if prompt_count % 2 == 0 else 1
    chunk = token_count // chunk_count
    prompts_per_chunk = prompt_count // chunk_count
    patched_chunks = []
    for index in range(chunk_count):
        prompts_here = slice(index * prompts_per_chunk, (index + 1) * prompts_per_chunk)
        placed = jnp.einsum(
            "jkr,jkd->jrd",
            pick_values[prompts_here],
            incoming[prompts_here],
            preferred_element_type=jnp.float32,
        ).astype(jnp.bfloat16)
        patched_here = jnp.where(
            patch_mask[prompts_here][..., None], placed, flat_heads[prompts_here]
        )
        patched_chunks.append(patched_here.reshape(chunk, -1))
    labels = concept_labels.reshape(token_count)
    concepts = probe_weight.shape[1]
    tensor_bits = [1 << k for k in range(lax.axis_size("tensor").bit_length() - 1)]
    halves, sent_block = [], None
    for index in range(chunk_count):
        rows_here = slice(index * chunk, (index + 1) * chunk)
        heads_here, sent_block, from_far = far_half(
            patched_chunks[index], out_weight, "tensor", sent_block
        )
        halves.append((heads_here, sent_block, from_far))
    attn_chunks, logit_chunks, grad_local = [], [], None
    for index in range(chunk_count):
        rows_here = slice(index * chunk, (index + 1) * chunk)
        heads_here, _, from_far = halves[index]
        if index + 1 < chunk_count:
            from_far, _ = lax.optimization_barrier((from_far, halves[index + 1][1]))
        attn_local = near_half(heads_here, out_weight, "tensor", from_far).astype(jnp.bfloat16)
        hidden = flat_residual[rows_here].astype(jnp.float32) + attn_local.astype(jnp.float32)
        square_local = jnp.sum(hidden * hidden, axis=1)
        scaled = hidden * norm_gain
        raw_part = jnp.dot(
            scaled, probe_weight, precision=lax.Precision.HIGH, preferred_element_type=jnp.float32
        )
        packed = jnp.concatenate([raw_part, square_local[:, None]], axis=1)
        packed = butterfly_sum(packed, "tensor", tensor_bits)
        inverse_rms = lax.rsqrt(packed[:, concepts] / DW + norm_epsilon)
        logits = packed[:, :concepts] * inverse_rms[:, None]
        normed = scaled * inverse_rms[:, None]
        classes = jnp.arange(concepts, dtype=jnp.int32)
        target = (labels[rows_here][:, None] == classes[None, :]).astype(jnp.float32)
        error = jax.nn.sigmoid(logits) - target
        grad_part = lax.dot_general(
            normed,
            error,
            (((0,), (0,)), ((), ())),
            precision=lax.Precision.HIGH,
            preferred_element_type=jnp.float32,
        )
        grad_local = grad_part if grad_local is None else grad_local + grad_part
        attn_chunks.append(attn_local)
        logit_chunks.append(logits)
    attn_local = jnp.concatenate(attn_chunks, axis=0)
    logits = jnp.concatenate(logit_chunks, axis=0)
    total_tokens = token_count * lax.axis_size("dp")
    grad_local = grad_local / math.sqrt(total_tokens)
    halving_bits, doubling_bits = dp_bits(lax.axis_size("dp"))
    probe_grad = tree_all_reduce(grad_local, "dp", halving_bits, doubling_bits)
    return (
        attn_local.reshape(prompt_count, seq_length, feature_count),
        logits.reshape(prompt_count, seq_length, -1),
        probe_grad,
    )


def solution(mesh):
    return jax.shard_map(
        per_device,
        mesh=mesh,
        in_specs=(
            P("dp", None, "tensor"),
            P("dp", None, "tensor"),
            P("dp", None, "tensor"),
            P("dp", None, "tensor"),
            P("tensor", None),
            P("tensor"),
            P("tensor", None),
            P("dp"),
            P("dp", "tensor", None),
            P("dp", None),
        ),
        out_specs=(P("dp", None, "tensor"), P("dp", None, None), P("tensor", None)),
        check_vma=False,
    )
```
